128 devices in a mesh: space: 8 (over x_hi, z), obs: 16 (over y, x_lo, core).
Axes of the slice: x: 4 (x_hi: 2, x_lo: 2; x = x_hi * 2 + x_lo), y: 4, z: 4, core: 2. Of those that a mesh axis runs over, the one named last changes fastest.
Arguments:
- pressure: float32 [256, 512, 256], P('space', 'obs'), may hold values from -6 to 6
- diffusion: float32 [256, 512, 256], P('space', 'obs'), may hold values from 0.02 to 0.15
- panel_cell: int32 [32768], P(('space', 'obs')), may hold values from 0 to 262143, as said below
- history: bfloat16 [32768, 2048], P(('space', 'obs')), may hold values from -6 to 6
- amplitude: bfloat16 [2048, 32768], P(None, ('space', 'obs')), may hold values from -0.125 to 0.125
- band_start: int32 [128, 16], P(('space', 'obs')), may hold values from 0 to 511
- interp_taps: float32 [4, 128, 16], P(None, ('space', 'obs')), may hold values from 0.1 to 0.6
Outputs:
- pressure_next: float32 [256, 512, 256], P('space', 'obs')
- panel_now: bfloat16 [32768], P(('space', 'obs'))
- spectra: float32 [2, 2048, 1024], P(None, ('space', 'obs'))
The draws below stay inside these ranges and needn't reach their ends.
Inputs may be any that keep to these rules, and one draw needn't show every extreme that they name: `panel_cell`: each entry is a cell of the brick of the device that holds the panel, numbered as in the reference program.
All inputs are finite; a program needn't handle non-finite values.
Results may differ from the reference program's by a relative error of at most 0.001.
Values sent between devices are 32-bit elements; how exact they have to be, the bound alone decides.
No kernel may reach another device: no remote copies, remote signals or barrier semaphores. Data moves between devices by JAX's collectives and lax.ppermute only.
A program may use at most 128 MiB of HBM per device.

```python
import math
import jax
import jax.numpy as jnp
from jax import lax

CX = 32
CY = 32
CZ = 256
PAN_DEV = 256
TS = 2048
BAND = 4
SMAX = 512
PB = 256
OB = 128
NX = 256
NY = 512
NZ = 256
PANELS = 32768
OBS = 2048
PAN_BLOCKS = 128
OBS_BLOCKS = 16
NF = 1024
N_OBS = 16


def draw_panel_cell(key, part):
    first_key, second_key = jax.random.split(jax.random.fold_in(key, 11), 2)
    cells = jax.random.randint(first_key, (PANELS,), 0, CX * CY * CZ, dtype=jnp.int32)
    where_top = jax.random.randint(second_key, (), 0, PANELS, dtype=jnp.int32)
    where_low = (where_top + PANELS // 2) % PANELS
    cells = cells.at[where_top].set(CX * CY * CZ - 1)
    return cells.at[where_low].set(0)


def draw_band_start(key, part):
    first_key, second_key = jax.random.split(jax.random.fold_in(key, 23), 2)
    entries = PAN_BLOCKS * OBS_BLOCKS
    delays = jax.random.randint(first_key, (entries,), 0, SMAX, dtype=jnp.int32)
    where_top = jax.random.randint(second_key, (), 0, entries, dtype=jnp.int32)
    where_low = (where_top + entries // 2) % entries
    delays = delays.at[where_top].set(SMAX - 1)
    delays = delays.at[where_low].set(0)
    return delays.reshape(PAN_BLOCKS, OBS_BLOCKS)


def spiked(array, own_key, source, target, blocks, factor):
    def block_of(dim):
        return (jnp.arange(array.shape[dim]) // (array.shape[dim] // blocks)).reshape((-1,) + (1,) * (array.ndim - 1 - dim))

    near = jax.random.permutation(own_key, blocks)[block_of(target)]
    far = (block_of(target) + blocks // 2) % blocks
    return jnp.where((block_of(source) == near) | (block_of(source) == far), factor * array, array)


def level_of(rng, shape, cuts, least, largest):
    def one(position, blocks):
        steps = jax.random.uniform(jax.random.fold_in(jax.random.fold_in(rng, 6), position), (blocks,), jnp.float32, least / len(cuts), largest / len(cuts))
        return jnp.repeat(jnp.exp(steps), shape[position] // blocks).reshape((-1,) + (1,) * (len(shape) - position - 1))

    loudness = one(*cuts[0])
    for cut in cuts[1:]:
        loudness = loudness * one(*cut)
    return loudness


def centred(rng, dims, scale, reach, pieces=(), kind=jnp.bfloat16):
    array = jax.random.normal(rng, dims, jnp.float32) * scale
    if len(pieces) > 0:
        array = level_of(rng, dims, pieces, -0.22, 0.18) * array
    return jnp.clip(array, min=-reach, max=reach).astype(kind)


def gaussian_with(key, shape, spread, most, cuts, heavy, held_as=jnp.bfloat16):
    result = spread * jax.random.normal(key, shape, jnp.float32)
    if cuts:
        result = result * level_of(key, shape, cuts, -0.22, 0.18)
    return jnp.clip(spiked(result, jax.random.fold_in(key, 3), *heavy), -most, most).astype(held_as)


def setup_inputs(seed: int = 0) -> dict:
    key_of = jax.random.split(jax.random.key(seed), 8)
    pressure = centred(key_of[0], (NX, NY, NZ), 1.0, 6.0, ((0, 8), (1, 16)), jnp.float32)
    diffusion = jnp.clip(0.02 + 0.13000001 * jax.random.uniform(key_of[1], (NX, NY, NZ), jnp.float32) ** level_of(key_of[1], (NX, NY, NZ), ((0, 8), (1, 16)), -0.2, 0.2), 0.02, 0.15)
    panel_cell = draw_panel_cell(jax.random.fold_in(key_of[7], 71), 0)
    history = centred(key_of[3], (PANELS, TS), 1.0, 6.0, ((0, 128),))
    amplitude = gaussian_with(key_of[4], (OBS, PANELS), PANELS ** -0.5, 0.125, ((1, 128),), (1, 0, 128, 5.5))
    band_start = draw_band_start(jax.random.fold_in(key_of[7], 71), 0)
    interp_taps = jnp.clip(0.1 + 0.5 * jax.random.uniform(key_of[6], (BAND, PAN_BLOCKS, OBS_BLOCKS), jnp.float32) ** level_of(key_of[6], (BAND, PAN_BLOCKS, OBS_BLOCKS), ((1, 128),), -0.2, 0.2), 0.1, 0.6)
    return {"pressure": pressure, "diffusion": diffusion, "panel_cell": panel_cell, "history": history, "amplitude": amplitude, "band_start": band_start, "interp_taps": interp_taps}


def integer_index(value):
    return jnp.asarray(value).astype(jnp.int32)

def operator(extended, diffusion):
    center = extended[1:-1, 1:-1, :]
    eastward = extended[2:, 1:-1, :]
    westward = extended[:-2, 1:-1, :]
    northward = extended[1:-1, 2:, :]
    southward = extended[1:-1, :-2, :]
    z_padded = jnp.pad(center, ((0, 0), (0, 0), (1, 1)))
    upward = z_padded[:, :, 2:]
    downward = z_padded[:, :, :-2]
    laplace = eastward + westward + northward + southward + upward + downward - 6.0 * center
    return diffusion * laplace - 0.25 * (eastward - westward)

def reference(pressure, diffusion, panel_cell, history, amplitude, band_start, interp_taps):
    extended = jnp.pad(pressure, ((1, 1), (1, 1), (0, 0)))
    section = pressure + operator(extended, diffusion)
    extended_section = jnp.pad(section, ((1, 1), (1, 1), (0, 0)))
    pressure_next = 0.5 * (pressure + (section + operator(extended_section, diffusion)))
    panel_ids = jnp.arange(PANELS, dtype=jnp.int32)
    device_ids = panel_ids // PAN_DEV
    space_ids = device_ids // N_OBS
    group_ids = device_ids % N_OBS
    cell_x = space_ids * CX + panel_cell // (CY * CZ)
    cell_y = group_ids * CY + panel_cell // CZ % CY
    cell_z = panel_cell % CZ
    panel_now = pressure_next[cell_x, cell_y, cell_z].astype(jnp.bfloat16)
    signals = jnp.concatenate([history[:, 1:], panel_now[:, None]], axis=1)

    def observer_block(obs_block):

        def add_panels(summed, panel_block):
            amp_block = lax.dynamic_slice(amplitude, (integer_index(obs_block * OB), integer_index(panel_block * PB)), (OB, PB)).astype(jnp.float32)
            sig_block = lax.dynamic_slice(signals, (integer_index(panel_block * PB), integer_index(0)), (PB, TS)).astype(jnp.float32)
            emitted = jnp.dot(amp_block, sig_block, precision=lax.Precision.HIGHEST)
            padded = jnp.concatenate([emitted, jnp.zeros((OB, SMAX + BAND), jnp.float32)], axis=1)
            begin_at = integer_index(band_start[panel_block, obs_block])
            for tap_index in range(BAND):
                moved = lax.dynamic_slice(padded, (integer_index(0), integer_index(begin_at + tap_index)), (OB, TS))
                summed = summed + interp_taps[tap_index, panel_block, obs_block] * moved
            return (summed, None)
        summed, _ = lax.scan(add_panels, jnp.zeros((OB, TS), jnp.float32), jnp.arange(PAN_BLOCKS, dtype=jnp.int32))
        return summed
    blocks = lax.map(observer_block, jnp.arange(OBS_BLOCKS, dtype=jnp.int32))
    signal = blocks.reshape(OBS, TS)
    window = 0.5 - 0.5 * jnp.cos(2.0 * math.pi * jnp.arange(TS, dtype=jnp.float32) / TS)
    transformed = jnp.fft.rfft(signal * window[None, :], axis=1)[:, :NF] / math.sqrt(TS)
    spectra = jnp.stack([jnp.real(transformed), jnp.imag(transformed)]).astype(jnp.float32)
    return (pressure_next, panel_now, spectra)
```

```python
import math

import jax
import jax.numpy as jnp
from jax import lax
from jax.experimental import pallas as pl
from jax.experimental.pallas import tpu as pltpu
from jax.sharding import PartitionSpec as P

TS = 2048
BAND = 4
SMAX = 512
OB = 128
NF = 1024
PADR = SMAX + 16
ROWS = 256
T1 = 32
T0 = TS // T1


def with_halo(cells, sides, width):
    for axis, dim in sides:
        count = lax.axis_size(axis)
        ends = count - 1
        head = lax.slice_in_dim(cells, 0, width, axis=dim)
        tail = lax.slice_in_dim(cells, cells.shape[dim] - width, cells.shape[dim], axis=dim)
        cells = jnp.concatenate(
            [
                lax.ppermute(tail, axis, [(i, (i + 1) % count) for i in range(ends)]),
                cells,
                lax.ppermute(head, axis, [((i + 1) % count, i) for i in range(ends)]),
            ],
            axis=dim,
        )
    return cells


def operator(extended, diffusion):
    center = extended[1:-1, 1:-1, :]
    eastward = extended[2:, 1:-1, :]
    westward = extended[:-2, 1:-1, :]
    northward = extended[1:-1, 2:, :]
    southward = extended[1:-1, :-2, :]
    z_padded = jnp.pad(center, ((0, 0), (0, 0), (1, 1)))
    upward = z_padded[:, :, 2:]
    downward = z_padded[:, :, :-2]
    laplace = eastward + westward + northward + southward + upward + downward - 6.0 * center
    return diffusion * laplace - 0.25 * (eastward - westward)


def section_faces(field):
    return with_halo(field, (("space", 0), ("obs", 1)), 1)


def shift_kernel(bs_ref, taps_ref, et_ref, out_ref, pad_ref):
    j = pl.program_id(0)
    begin = bs_ref[j]
    pad_ref[pl.ds(0, TS), :] = et_ref[...]
    pad_ref[pl.ds(TS, PADR), :] = jnp.zeros((PADR, OB), jnp.float32)
    weights = [taps_ref[k, j] for k in range(BAND)]
    for r in range(TS // ROWS):
        acc = weights[0] * pad_ref[pl.ds(begin + r * ROWS, ROWS), :]
        for k in range(1, BAND):
            acc = acc + weights[k] * pad_ref[pl.ds(begin + k + r * ROWS, ROWS), :]
        out_ref[:, pl.ds(r * ROWS, ROWS)] = acc.T


def shifted_partial(et, band_row, taps):
    blocks = et.shape[1] // OB
    return pl.pallas_call(
        shift_kernel,
        grid_spec=pltpu.PrefetchScalarGridSpec(
            num_scalar_prefetch=1,
            grid=(blocks,),
            in_specs=[
                pl.BlockSpec(memory_space=pltpu.SMEM),
                pl.BlockSpec((TS, OB), lambda j, bs: (0, j)),
            ],
            out_specs=pl.BlockSpec((OB, TS), lambda j, bs: (j, 0)),
            scratch_shapes=[pltpu.VMEM((TS + PADR, OB), jnp.float32)],
        ),
        out_shape=jax.ShapeDtypeStruct((et.shape[1], TS), jnp.float32),
    )(band_row, taps, et)


def dft(windowed):
    n = windowed.shape[0]
    f_ids = jnp.arange(NF, dtype=jnp.int32)
    t0_ids = jnp.arange(T0, dtype=jnp.int32)
    t1_ids = jnp.arange(T1, dtype=jnp.int32)
    scale = 2.0 * math.pi / TS
    inner = (t0_ids[:, None] * f_ids[None, :] % TS).astype(jnp.float32) * scale
    outer = (t1_ids[:, None] * T0 * f_ids[None, :] % TS).astype(jnp.float32) * scale
    cos_in, sin_in = jnp.cos(inner), jnp.sin(inner)
    cos_out, sin_out = jnp.cos(outer), jnp.sin(outer)
    split = windowed.reshape(n * T1, T0)
    u_cos = jnp.dot(split, cos_in, precision=lax.Precision.HIGHEST).reshape(n, T1, NF)
    u_sin = jnp.dot(split, sin_in, precision=lax.Precision.HIGHEST).reshape(n, T1, NF)
    real_part = jnp.sum(cos_out[None] * u_cos - sin_out[None] * u_sin, axis=1)
    imag_part = -jnp.sum(sin_out[None] * u_cos + cos_out[None] * u_sin, axis=1)
    root = math.sqrt(TS)
    return jnp.stack([real_part / root, imag_part / root])


def on_device(pressure, diffusion, panel_cell, history, amplitude, band_start, interp_taps):
    axes = ("space", "obs")
    me = lax.axis_index("space") * lax.axis_size("obs") + lax.axis_index("obs")
    devices = lax.axis_size("space") * lax.axis_size("obs")
    obs_total = amplitude.shape[0]
    own = obs_total // devices

    shifted = jnp.concatenate([history[:, 1:], jnp.zeros_like(history[:, :1])], axis=1)
    et = lax.dot_general(
        shifted, amplitude, (((0,), (1,)), ((), ())), preferred_element_type=jnp.float32
    )
    partial = shifted_partial(et, band_start[0], interp_taps[:, 0, :])
    series = lax.psum_scatter(partial, axes, scatter_dimension=0, tiled=True)

    section = pressure + operator(section_faces(pressure), diffusion)
    pressure_next = 0.5 * (pressure + (section + operator(section_faces(section), diffusion)))
    panel_now = jnp.take(pressure_next.reshape(-1), panel_cell).astype(jnp.bfloat16)

    newest = jnp.dot(amplitude, panel_now, preferred_element_type=jnp.float32)
    newest = lax.all_to_all(newest.reshape(devices, own), axes, 0, 0, tiled=True)
    starts = lax.all_gather(band_start.astype(jnp.float32), axes, axis=0, tiled=True)
    weights = lax.all_gather(interp_taps, axes, axis=1, tiled=True)
    block = (me * own) // OB
    my_starts = lax.dynamic_index_in_dim(starts, block, axis=1, keepdims=False).astype(jnp.int32)
    my_weights = lax.dynamic_index_in_dim(weights, block, axis=2, keepdims=False)
    t_ids = jnp.arange(TS, dtype=jnp.int32)
    spread = jnp.zeros((devices, TS), jnp.float32)
    for tap_index in range(BAND):
        hit = t_ids[None, :] == (TS - 1 - tap_index - my_starts)[:, None]
        spread = spread + jnp.where(hit, my_weights[tap_index][:, None], 0.0)
    series = series + lax.dot_general(
        newest, spread, (((0,), (0,)), ((), ())), precision=lax.Precision.HIGHEST
    )

    window = 0.5 - 0.5 * jnp.cos(2.0 * math.pi * jnp.arange(TS, dtype=jnp.float32) / TS)
    spectra = dft(series * window[None, :])
    return (pressure_next, panel_now, spectra)


def solution(mesh):
    in_specs = (
        P("space", "obs", None),
        P("space", "obs", None),
        P(("space", "obs")),
        P(("space", "obs"), None),
        P(None, ("space", "obs")),
        P(("space", "obs"), None),
        P(None, ("space", "obs"), None),
    )
    out_specs = (P("space", "obs", None), P(("space", "obs")), P(None, ("space", "obs"), None))
    return jax.shard_map(
        on_device, mesh=mesh, in_specs=in_specs, out_specs=out_specs, check_vma=False
    )
```

```python
import math

import jax
import jax.numpy as jnp
from jax import lax
from jax.experimental import pallas as pl
from jax.experimental.pallas import tpu as pltpu
from jax.sharding import PartitionSpec as P

TS = 2048
BAND = 4
SMAX = 512
OB = 128
NF = 1024
PADR = SMAX + 16
ROWS = 256
T1 = 32
T0 = TS // T1


def with_halo(cells, sides, width):
    for axis, dim in sides:
        count = lax.axis_size(axis)
        ends = count - 1
        head = lax.slice_in_dim(cells, 0, width, axis=dim)
        tail = lax.slice_in_dim(cells, cells.shape[dim] - width, cells.shape[dim], axis=dim)
        cells = jnp.concatenate(
            [
                lax.ppermute(tail, axis, [(i, (i + 1) % count) for i in range(ends)]),
                cells,
                lax.ppermute(head, axis, [((i + 1) % count, i) for i in range(ends)]),
            ],
            axis=dim,
        )
    return cells


def operator(extended, diffusion):
    center = extended[1:-1, 1:-1, :]
    eastward = extended[2:, 1:-1, :]
    westward = extended[:-2, 1:-1, :]
    northward = extended[1:-1, 2:, :]
    southward = extended[1:-1, :-2, :]
    z_padded = jnp.pad(center, ((0, 0), (0, 0), (1, 1)))
    upward = z_padded[:, :, 2:]
    downward = z_padded[:, :, :-2]
    laplace = eastward + westward + northward + southward + upward + downward - 6.0 * center
    return diffusion * laplace - 0.25 * (eastward - westward)


def section_faces(field):
    return with_halo(field, (("space", 0), ("obs", 1)), 1)


def shift_kernel(bs_ref, taps_ref, et_ref, out_ref, pad_ref):
    j = pl.program_id(0)
    begin = bs_ref[j]
    pad_ref[pl.ds(0, TS), :] = et_ref[...]
    pad_ref[pl.ds(TS, PADR), :] = jnp.zeros((PADR, OB), jnp.float32)
    weights = [taps_ref[k, j] for k in range(BAND)]
    for r in range(TS // ROWS):
        acc = weights[0] * pad_ref[pl.ds(begin + r * ROWS, ROWS), :]
        for k in range(1, BAND):
            acc = acc + weights[k] * pad_ref[pl.ds(begin + k + r * ROWS, ROWS), :]
        out_ref[:, pl.ds(r * ROWS, ROWS)] = acc.T


def shifted_partial(et, band_row, taps):
    blocks = et.shape[1] // OB
    return pl.pallas_call(
        shift_kernel,
        grid_spec=pltpu.PrefetchScalarGridSpec(
            num_scalar_prefetch=1,
            grid=(blocks,),
            in_specs=[
                pl.BlockSpec(memory_space=pltpu.SMEM),
                pl.BlockSpec((TS, OB), lambda j, bs: (0, j)),
            ],
            out_specs=pl.BlockSpec((OB, TS), lambda j, bs: (j, 0)),
            scratch_shapes=[pltpu.VMEM((TS + PADR, OB), jnp.float32)],
        ),
        out_shape=jax.ShapeDtypeStruct((et.shape[1], TS), jnp.float32),
    )(band_row, taps, et)


def dft(windowed):
    n = windowed.shape[0]
    f_ids = jnp.arange(NF, dtype=jnp.int32)
    t0_ids = jnp.arange(T0, dtype=jnp.int32)
    t1_ids = jnp.arange(T1, dtype=jnp.int32)
    scale = 2.0 * math.pi / TS
    inner = (t0_ids[:, None] * f_ids[None, :] % TS).astype(jnp.float32) * scale
    outer = (t1_ids[:, None] * T0 * f_ids[None, :] % TS).astype(jnp.float32) * scale
    cos_in, sin_in = jnp.cos(inner), jnp.sin(inner)
    cos_out, sin_out = jnp.cos(outer), jnp.sin(outer)
    split = windowed.reshape(n * T1, T0)
    u_cos = jnp.dot(split, cos_in, precision=lax.Precision.HIGHEST).reshape(n, T1, NF)
    u_sin = jnp.dot(split, sin_in, precision=lax.Precision.HIGHEST).reshape(n, T1, NF)
    real_part = jnp.sum(cos_out[None] * u_cos - sin_out[None] * u_sin, axis=1)
    imag_part = -jnp.sum(sin_out[None] * u_cos + cos_out[None] * u_sin, axis=1)
    root = math.sqrt(TS)
    return jnp.stack([real_part / root, imag_part / root])


def on_device(pressure, diffusion, panel_cell, history, amplitude, band_start, interp_taps):
    axes = ("space", "obs")
    devices = lax.axis_size("space") * lax.axis_size("obs")
    obs_total = amplitude.shape[0]
    own = obs_total // devices

    shifted = jnp.concatenate([history[:, 1:], jnp.zeros_like(history[:, :1])], axis=1)
    et = lax.dot_general(
        shifted, amplitude, (((0,), (1,)), ((), ())), preferred_element_type=jnp.float32
    )
    partial = shifted_partial(et, band_start[0], interp_taps[:, 0, :])
    time_share = lax.psum_scatter(partial, "obs", scatter_dimension=1, tiled=True)
    owner_share = lax.psum_scatter(time_share, "space", scatter_dimension=0, tiled=True)
    series = lax.all_to_all(owner_share, "obs", split_axis=0, concat_axis=1, tiled=True)

    section = pressure + operator(section_faces(pressure), diffusion)
    pressure_next = 0.5 * (pressure + (section + operator(section_faces(section), diffusion)))
    panel_now = jnp.take(pressure_next.reshape(-1), panel_cell).astype(jnp.bfloat16)

    newest = jnp.dot(amplitude, panel_now, preferred_element_type=jnp.float32).reshape(devices, own)
    per_owner = OB // own
    owner_taps = jnp.repeat(interp_taps[:, 0, :], per_owner, axis=1)
    owner_starts = jnp.repeat(band_start[0].astype(jnp.float32), per_owner)
    payload = jnp.concatenate(
        [
            owner_taps.T[:, :, None] * newest[:, None, :],
            jnp.broadcast_to(owner_starts[:, None, None], (devices, 1, own)),
        ],
        axis=1,
    )
    arrived = lax.all_to_all(payload, axes, 0, 0, tiled=True)
    their_starts = arrived[:, BAND, 0].astype(jnp.int32)
    t_ids = jnp.arange(TS, dtype=jnp.int32)
    for tap_index in range(BAND):
        hit = t_ids[None, :] == (TS - 1 - tap_index - their_starts)[:, None]
        series = series + lax.dot_general(
            arrived[:, tap_index, :],
            hit.astype(jnp.float32),
            (((0,), (0,)), ((), ())),
            precision=lax.Precision.HIGHEST,
        )

    window = 0.5 - 0.5 * jnp.cos(2.0 * math.pi * jnp.arange(TS, dtype=jnp.float32) / TS)
    spectra = dft(series * window[None, :])
    return (pressure_next, panel_now, spectra)


def solution(mesh):
    in_specs = (
        P("space", "obs", None),
        P("space", "obs", None),
        P(("space", "obs")),
        P(("space", "obs"), None),
        P(None, ("space", "obs")),
        P(("space", "obs"), None),
        P(None, ("space", "obs"), None),
    )
    out_specs = (P("space", "obs", None), P(("space", "obs")), P(None, ("space", "obs"), None))
    return jax.shard_map(
        on_device, mesh=mesh, in_specs=in_specs, out_specs=out_specs, check_vma=False
    )
```

```python
import math

import jax
import jax.numpy as jnp
from jax import lax
from jax.experimental import pallas as pl
from jax.experimental.pallas import tpu as pltpu
from jax.sharding import PartitionSpec as P

TS = 2048
BAND = 4
SMAX = 512
OB = 128
NF = 1024
PADR = SMAX + 16
ROWS = 256
T1 = 32
T0 = TS // T1


def with_halo(cells, sides, width):
    for axis, dim in sides:
        count = lax.axis_size(axis)
        ends = count - 1
        head = lax.slice_in_dim(cells, 0, width, axis=dim)
        tail = lax.slice_in_dim(cells, cells.shape[dim] - width, cells.shape[dim], axis=dim)
        cells = jnp.concatenate(
            [
                lax.ppermute(tail, axis, [(i, (i + 1) % count) for i in range(ends)]),
                cells,
                lax.ppermute(head, axis, [((i + 1) % count, i) for i in range(ends)]),
            ],
            axis=dim,
        )
    return cells


def operator(extended, diffusion):
    center = extended[1:-1, 1:-1, :]
    eastward = extended[2:, 1:-1, :]
    westward = extended[:-2, 1:-1, :]
    northward = extended[1:-1, 2:, :]
    southward = extended[1:-1, :-2, :]
    z_padded = jnp.pad(center, ((0, 0), (0, 0), (1, 1)))
    upward = z_padded[:, :, 2:]
    downward = z_padded[:, :, :-2]
    laplace = eastward + westward + northward + southward + upward + downward - 6.0 * center
    return diffusion * laplace - 0.25 * (eastward - westward)


def section_faces(field):
    return with_halo(field, (("space", 0), ("obs", 1)), 1)


def shift_kernel(bs_ref, taps_ref, et_ref, out_ref, pad_ref):
    j = pl.program_id(0)
    begin = bs_ref[j]
    pad_ref[pl.ds(0, TS), :] = et_ref[...]
    pad_ref[pl.ds(TS, PADR), :] = jnp.zeros((PADR, OB), jnp.float32)
    weights = [taps_ref[k, j] for k in range(BAND)]
    for r in range(TS // ROWS):
        acc = weights[0] * pad_ref[pl.ds(begin + r * ROWS, ROWS), :]
        for k in range(1, BAND):
            acc = acc + weights[k] * pad_ref[pl.ds(begin + k + r * ROWS, ROWS), :]
        out_ref[:, pl.ds(r * ROWS, ROWS)] = acc.T


def shifted_partial(et, band_row, taps):
    blocks = et.shape[1] // OB
    return pl.pallas_call(
        shift_kernel,
        grid_spec=pltpu.PrefetchScalarGridSpec(
            num_scalar_prefetch=1,
            grid=(blocks,),
            in_specs=[
                pl.BlockSpec(memory_space=pltpu.SMEM),
                pl.BlockSpec((TS, OB), lambda j, bs: (0, j)),
            ],
            out_specs=pl.BlockSpec((OB, TS), lambda j, bs: (j, 0)),
            scratch_shapes=[pltpu.VMEM((TS + PADR, OB), jnp.float32)],
        ),
        out_shape=jax.ShapeDtypeStruct((et.shape[1], TS), jnp.float32),
    )(band_row, taps, et)


def dft(windowed):
    n = windowed.shape[0]
    f_ids = jnp.arange(NF, dtype=jnp.int32)
    t0_ids = jnp.arange(T0, dtype=jnp.int32)
    t1_ids = jnp.arange(T1, dtype=jnp.int32)
    scale = 2.0 * math.pi / TS
    inner = (t0_ids[:, None] * f_ids[None, :] % TS).astype(jnp.float32) * scale
    outer = (t1_ids[:, None] * T0 * f_ids[None, :] % TS).astype(jnp.float32) * scale
    cos_in, sin_in = jnp.cos(inner), jnp.sin(inner)
    cos_out, sin_out = jnp.cos(outer), jnp.sin(outer)
    split = windowed.reshape(n * T1, T0)
    u_cos = jnp.dot(split, cos_in, precision=lax.Precision.HIGHEST).reshape(n, T1, NF)
    u_sin = jnp.dot(split, sin_in, precision=lax.Precision.HIGHEST).reshape(n, T1, NF)
    real_part = jnp.sum(cos_out[None] * u_cos - sin_out[None] * u_sin, axis=1)
    imag_part = -jnp.sum(sin_out[None] * u_cos + cos_out[None] * u_sin, axis=1)
    root = math.sqrt(TS)
    return jnp.stack([real_part / root, imag_part / root])


def on_device(pressure, diffusion, panel_cell, history, amplitude, band_start, interp_taps):
    axes = ("space", "obs")
    devices = lax.axis_size("space") * lax.axis_size("obs")
    obs_total = amplitude.shape[0]
    own = obs_total // devices

    shifted = jnp.concatenate([history[:, 1:], jnp.zeros_like(history[:, :1])], axis=1)
    et = lax.dot_general(
        shifted, amplitude, (((0,), (1,)), ((), ())), preferred_element_type=jnp.float32
    )
    partial = shifted_partial(et, band_start[0], interp_taps[:, 0, :])
    time_share = lax.psum_scatter(partial, "obs", scatter_dimension=1, tiled=True)
    groups = lax.axis_size("space")
    pieces = time_share.reshape(groups, obs_total // groups, time_share.shape[1])
    owner_share = jnp.sum(lax.all_to_all(pieces, "space", 0, 0, tiled=True), axis=0)
    series = lax.all_to_all(owner_share, "obs", split_axis=0, concat_axis=1, tiled=True)

    section = pressure + operator(section_faces(pressure), diffusion)
    pressure_next = 0.5 * (pressure + (section + operator(section_faces(section), diffusion)))
    panel_now = jnp.take(pressure_next.reshape(-1), panel_cell).astype(jnp.bfloat16)

    newest = jnp.dot(amplitude, panel_now, preferred_element_type=jnp.float32).reshape(devices, own)
    per_owner = OB // own
    owner_taps = jnp.repeat(interp_taps[:, 0, :], per_owner, axis=1)
    owner_starts = jnp.repeat(band_start[0].astype(jnp.float32), per_owner)
    payload = jnp.concatenate(
        [
            owner_taps.T[:, :, None] * newest[:, None, :],
            jnp.broadcast_to(owner_starts[:, None, None], (devices, 1, own)),
        ],
        axis=1,
    )
    arrived = lax.all_to_all(payload, axes, 0, 0, tiled=True)
    their_starts = arrived[:, BAND, 0].astype(jnp.int32)
    t_ids = jnp.arange(TS, dtype=jnp.int32)
    for tap_index in range(BAND):
        hit = t_ids[None, :] == (TS - 1 - tap_index - their_starts)[:, None]
        series = series + lax.dot_general(
            arrived[:, tap_index, :],
            hit.astype(jnp.float32),
            (((0,), (0,)), ((), ())),
            precision=lax.Precision.HIGHEST,
        )

    window = 0.5 - 0.5 * jnp.cos(2.0 * math.pi * jnp.arange(TS, dtype=jnp.float32) / TS)
    spectra = dft(series * window[None, :])
    return (pressure_next, panel_now, spectra)


def solution(mesh):
    in_specs = (
        P("space", "obs", None),
        P("space", "obs", None),
        P(("space", "obs")),
        P(("space", "obs"), None),
        P(None, ("space", "obs")),
        P(("space", "obs"), None),
        P(None, ("space", "obs"), None),
    )
    out_specs = (P("space", "obs", None), P(("space", "obs")), P(None, ("space", "obs"), None))
    return jax.shard_map(
        on_device, mesh=mesh, in_specs=in_specs, out_specs=out_specs, check_vma=False
    )
```

```python
import math

import jax
import jax.numpy as jnp
from jax import lax
from jax.experimental import pallas as pl
from jax.experimental.pallas import tpu as pltpu
from jax.sharding import PartitionSpec as P

TS = 2048
BAND = 4
SMAX = 512
OB = 128
NF = 1024
PADR = SMAX + 16
ROWS = 256
T1 = 32
T0 = TS // T1


def with_halo(cells, sides, width):
    for axis, dim in sides:
        count = lax.axis_size(axis)
        ends = count - 1
        head = lax.slice_in_dim(cells, 0, width, axis=dim)
        tail = lax.slice_in_dim(cells, cells.shape[dim] - width, cells.shape[dim], axis=dim)
        cells = jnp.concatenate(
            [
                lax.ppermute(tail, axis, [(i, (i + 1) % count) for i in range(ends)]),
                cells,
                lax.ppermute(head, axis, [((i + 1) % count, i) for i in range(ends)]),
            ],
            axis=dim,
        )
    return cells


def operator(extended, diffusion):
    center = extended[1:-1, 1:-1, :]
    eastward = extended[2:, 1:-1, :]
    westward = extended[:-2, 1:-1, :]
    northward = extended[1:-1, 2:, :]
    southward = extended[1:-1, :-2, :]
    z_padded = jnp.pad(center, ((0, 0), (0, 0), (1, 1)))
    upward = z_padded[:, :, 2:]
    downward = z_padded[:, :, :-2]
    laplace = eastward + westward + northward + southward + upward + downward - 6.0 * center
    return diffusion * laplace - 0.25 * (eastward - westward)


def section_faces(field):
    return with_halo(field, (("space", 0), ("obs", 1)), 1)


def shift_kernel(bs_ref, taps_ref, own_ref, other_ref, out_ref, own_pad, other_pad):
    j = pl.program_id(0)
    for pad_ref, et_ref in ((own_pad, own_ref), (other_pad, other_ref)):
        pad_ref[pl.ds(0, TS), :] = et_ref[...]
        pad_ref[pl.ds(TS, PADR), :] = jnp.zeros((PADR, OB), jnp.float32)
    begins = [bs_ref[0, j], bs_ref[1, j]]
    weights = [[taps_ref[src, k, j] for k in range(BAND)] for src in range(2)]
    for r in range(TS // ROWS):
        acc = None
        for src, pad_ref in enumerate((own_pad, other_pad)):
            for k in range(BAND):
                term = weights[src][k] * pad_ref[pl.ds(begins[src] + k + r * ROWS, ROWS), :]
                acc = term if acc is None else acc + term
        out_ref[:, pl.ds(r * ROWS, ROWS)] = acc.T


def shifted_partial(own_et, other_et, band_rows, taps):
    blocks = own_et.shape[1] // OB
    block_spec = pl.BlockSpec((TS, OB), lambda j, bs: (0, j))
    return pl.pallas_call(
        shift_kernel,
        grid_spec=pltpu.PrefetchScalarGridSpec(
            num_scalar_prefetch=1,
            grid=(blocks,),
            in_specs=[pl.BlockSpec(memory_space=pltpu.SMEM), block_spec, block_spec],
            out_specs=pl.BlockSpec((OB, TS), lambda j, bs: (j, 0)),
            scratch_shapes=[
                pltpu.VMEM((TS + PADR, OB), jnp.float32),
                pltpu.VMEM((TS + PADR, OB), jnp.float32),
            ],
        ),
        out_shape=jax.ShapeDtypeStruct((own_et.shape[1], TS), jnp.float32),
    )(band_rows, taps, own_et, other_et)


def dft(windowed):
    n = windowed.shape[0]
    f_ids = jnp.arange(NF, dtype=jnp.int32)
    t0_ids = jnp.arange(T0, dtype=jnp.int32)
    t1_ids = jnp.arange(T1, dtype=jnp.int32)
    scale = 2.0 * math.pi / TS
    inner = (t0_ids[:, None] * f_ids[None, :] % TS).astype(jnp.float32) * scale
    outer = (t1_ids[:, None] * T0 * f_ids[None, :] % TS).astype(jnp.float32) * scale
    cos_in, sin_in = jnp.cos(inner), jnp.sin(inner)
    cos_out, sin_out = jnp.cos(outer), jnp.sin(outer)
    split = windowed.reshape(n * T1, T0)
    u_cos = jnp.dot(split, cos_in, precision=lax.Precision.HIGHEST).reshape(n, T1, NF)
    u_sin = jnp.dot(split, sin_in, precision=lax.Precision.HIGHEST).reshape(n, T1, NF)
    real_part = jnp.sum(cos_out[None] * u_cos - sin_out[None] * u_sin, axis=1)
    imag_part = -jnp.sum(sin_out[None] * u_cos + cos_out[None] * u_sin, axis=1)
    root = math.sqrt(TS)
    return jnp.stack([real_part / root, imag_part / root])


def on_device(pressure, diffusion, panel_cell, history, amplitude, band_start, interp_taps):
    axes = ("space", "obs")
    devices = lax.axis_size("space") * lax.axis_size("obs")
    obs_total = amplitude.shape[0]
    own = obs_total // devices

    spaces = lax.axis_size("space")
    s_id = lax.axis_index("space")
    parity = s_id % 2
    swap = [(i, i ^ 1) for i in range(spaces)]
    quads = obs_total // (4 * OB)
    halves = amplitude.reshape(quads, 2, 2 * OB, amplitude.shape[1])
    own_rows = lax.dynamic_index_in_dim(halves, parity, axis=1, keepdims=False)
    other_rows = lax.dynamic_index_in_dim(halves, 1 - parity, axis=1, keepdims=False)
    own_rows = own_rows.reshape(obs_total // 2, amplitude.shape[1])
    other_rows = other_rows.reshape(obs_total // 2, amplitude.shape[1])
    shifted = jnp.concatenate([history[:, 1:], jnp.zeros_like(history[:, :1])], axis=1)
    nothing = 0.0 * interp_taps[0, 0, 0]
    got_signals = lax.ppermute(shifted.astype(jnp.float32), "space", swap)
    got_signals = (got_signals + nothing).astype(jnp.bfloat16)
    got_rows = lax.ppermute(other_rows.astype(jnp.float32), "space", swap)
    got_rows = (got_rows + nothing).astype(jnp.bfloat16)
    got_band = lax.ppermute(band_start[0].astype(jnp.float32), "space", swap).astype(jnp.int32)
    got_taps = lax.ppermute(interp_taps[:, 0, :], "space", swap)
    mine = jnp.arange(obs_total // (2 * OB), dtype=jnp.int32)
    mine = 4 * (mine // 2) + 2 * parity + mine % 2
    band_rows = jnp.stack([band_start[0][mine], got_band[mine]])
    tap_rows = jnp.stack([interp_taps[:, 0, :][:, mine], got_taps[:, mine]])
    contract = (((0,), (1,)), ((), ()))
    own_et = lax.dot_general(shifted, own_rows, contract, preferred_element_type=jnp.float32)
    other_et = lax.dot_general(got_signals, got_rows, contract, preferred_element_type=jnp.float32)
    partial = shifted_partial(own_et, other_et, band_rows, tap_rows)
    time_share = lax.psum_scatter(partial, "obs", scatter_dimension=1, tiled=True)
    quarter = time_share.reshape(quads, 2 * OB, time_share.shape[1])
    empty = jnp.zeros_like(quarter)
    pieces = jnp.where(
        parity == 0, jnp.stack([quarter, empty], axis=1), jnp.stack([empty, quarter], axis=1)
    ).reshape(spaces, 2 * OB, time_share.shape[1])
    owner_share = jnp.sum(lax.all_to_all(pieces, "space", 0, 0, tiled=True), axis=0)
    series = lax.all_to_all(owner_share, "obs", split_axis=0, concat_axis=1, tiled=True)

    section = pressure + operator(section_faces(pressure), diffusion)
    pressure_next = 0.5 * (pressure + (section + operator(section_faces(section), diffusion)))
    panel_now = jnp.take(pressure_next.reshape(-1), panel_cell).astype(jnp.bfloat16)

    newest = jnp.dot(amplitude, panel_now, preferred_element_type=jnp.float32).reshape(devices, own)
    per_owner = OB // own
    owner_taps = jnp.repeat(interp_taps[:, 0, :], per_owner, axis=1)
    owner_starts = jnp.repeat(band_start[0].astype(jnp.float32), per_owner)
    payload = jnp.concatenate(
        [
            owner_taps.T[:, :, None] * newest[:, None, :],
            jnp.broadcast_to(owner_starts[:, None, None], (devices, 1, own)),
        ],
        axis=1,
    )
    arrived = lax.all_to_all(payload, axes, 0, 0, tiled=True)
    their_starts = arrived[:, BAND, 0].astype(jnp.int32)
    t_ids = jnp.arange(TS, dtype=jnp.int32)
    for tap_index in range(BAND):
        hit = t_ids[None, :] == (TS - 1 - tap_index - their_starts)[:, None]
        series = series + lax.dot_general(
            arrived[:, tap_index, :],
            hit.astype(jnp.float32),
            (((0,), (0,)), ((), ())),
            precision=lax.Precision.HIGHEST,
        )

    window = 0.5 - 0.5 * jnp.cos(2.0 * math.pi * jnp.arange(TS, dtype=jnp.float32) / TS)
    spectra = dft(series * window[None, :])
    return (pressure_next, panel_now, spectra)


def solution(mesh):
    in_specs = (
        P("space", "obs", None),
        P("space", "obs", None),
        P(("space", "obs")),
        P(("space", "obs"), None),
        P(None, ("space", "obs")),
        P(("space", "obs"), None),
        P(None, ("space", "obs"), None),
    )
    out_specs = (P("space", "obs", None), P(("space", "obs")), P(None, ("space", "obs"), None))
    return jax.shard_map(
        on_device, mesh=mesh, in_specs=in_specs, out_specs=out_specs, check_vma=False
    )
```

```python
import math

import jax
import jax.numpy as jnp
from jax import lax
from jax.experimental import pallas as pl
from jax.experimental.pallas import tpu as pltpu
from jax.sharding import PartitionSpec as P

TS = 2048
BAND = 4
SMAX = 512
OB = 128
NF = 1024
PADR = SMAX + 16
ROWS = 256
T1 = 32
T0 = TS // T1


def with_halo(cells, sides, width):
    for axis, dim in sides:
        count = lax.axis_size(axis)
        ends = count - 1
        head = lax.slice_in_dim(cells, 0, width, axis=dim)
        tail = lax.slice_in_dim(cells, cells.shape[dim] - width, cells.shape[dim], axis=dim)
        cells = jnp.concatenate(
            [
                lax.ppermute(tail, axis, [(i, (i + 1) % count) for i in range(ends)]),
                cells,
                lax.ppermute(head, axis, [((i + 1) % count, i) for i in range(ends)]),
            ],
            axis=dim,
        )
    return cells


def operator(extended, diffusion):
    center = extended[1:-1, 1:-1, :]
    eastward = extended[2:, 1:-1, :]
    westward = extended[:-2, 1:-1, :]
    northward = extended[1:-1, 2:, :]
    southward = extended[1:-1, :-2, :]
    z_padded = jnp.pad(center, ((0, 0), (0, 0), (1, 1)))
    upward = z_padded[:, :, 2:]
    downward = z_padded[:, :, :-2]
    laplace = eastward + westward + northward + southward + upward + downward - 6.0 * center
    return diffusion * laplace - 0.25 * (eastward - westward)


def section_faces(field):
    return with_halo(field, (("space", 0), ("obs", 1)), 1)


def shift_kernel(bs_ref, taps_ref, own_ref, other_ref, out_ref, own_pad, other_pad):
    j = pl.program_id(0)
    for pad_ref, et_ref in ((own_pad, own_ref), (other_pad, other_ref)):
        pad_ref[pl.ds(0, TS), :] = et_ref[...]
        pad_ref[pl.ds(TS, PADR), :] = jnp.zeros((PADR, OB), jnp.float32)
    begins = [bs_ref[0, j], bs_ref[1, j]]
    weights = [[taps_ref[src, k, j] for k in range(BAND)] for src in range(2)]
    for r in range(TS // ROWS):
        acc = None
        for src, pad_ref in enumerate((own_pad, other_pad)):
            for k in range(BAND):
                term = weights[src][k] * pad_ref[pl.ds(begins[src] + k + r * ROWS, ROWS), :]
                acc = term if acc is None else acc + term
        out_ref[:, pl.ds(r * ROWS, ROWS)] = acc.T


def shifted_partial(own_et, other_et, band_rows, taps):
    blocks = own_et.shape[1] // OB
    block_spec = pl.BlockSpec((TS, OB), lambda j, bs: (0, j))
    return pl.pallas_call(
        shift_kernel,
        grid_spec=pltpu.PrefetchScalarGridSpec(
            num_scalar_prefetch=1,
            grid=(blocks,),
            in_specs=[pl.BlockSpec(memory_space=pltpu.SMEM), block_spec, block_spec],
            out_specs=pl.BlockSpec((OB, TS), lambda j, bs: (j, 0)),
            scratch_shapes=[
                pltpu.VMEM((TS + PADR, OB), jnp.float32),
                pltpu.VMEM((TS + PADR, OB), jnp.float32),
            ],
        ),
        out_shape=jax.ShapeDtypeStruct((own_et.shape[1], TS), jnp.float32),
    )(band_rows, taps, own_et, other_et)


def dft(windowed):
    n = windowed.shape[0]
    f_ids = jnp.arange(NF, dtype=jnp.int32)
    t0_ids = jnp.arange(T0, dtype=jnp.int32)
    t1_ids = jnp.arange(T1, dtype=jnp.int32)
    scale = 2.0 * math.pi / TS
    inner = (t0_ids[:, None] * f_ids[None, :] % TS).astype(jnp.float32) * scale
    outer = (t1_ids[:, None] * T0 * f_ids[None, :] % TS).astype(jnp.float32) * scale
    cos_in, sin_in = jnp.cos(inner), jnp.sin(inner)
    cos_out, sin_out = jnp.cos(outer), jnp.sin(outer)
    split = windowed.reshape(n * T1, T0)
    u_cos = jnp.dot(split, cos_in, precision=lax.Precision.HIGHEST).reshape(n, T1, NF)
    u_sin = jnp.dot(split, sin_in, precision=lax.Precision.HIGHEST).reshape(n, T1, NF)
    real_part = jnp.sum(cos_out[None] * u_cos - sin_out[None] * u_sin, axis=1)
    imag_part = -jnp.sum(sin_out[None] * u_cos + cos_out[None] * u_sin, axis=1)
    root = math.sqrt(TS)
    return jnp.stack([real_part / root, imag_part / root])


def on_device(pressure, diffusion, panel_cell, history, amplitude, band_start, interp_taps):
    axes = ("space", "obs")
    devices = lax.axis_size("space") * lax.axis_size("obs")
    obs_total = amplitude.shape[0]
    own = obs_total // devices

    spaces = lax.axis_size("space")
    s_id = lax.axis_index("space")
    parity = s_id % 2
    swap = [(i, i ^ 1) for i in range(spaces)]
    quads = obs_total // (4 * OB)
    halves = amplitude.reshape(quads, 2, 2 * OB, amplitude.shape[1])
    own_rows = lax.dynamic_index_in_dim(halves, parity, axis=1, keepdims=False)
    other_rows = lax.dynamic_index_in_dim(halves, 1 - parity, axis=1, keepdims=False)
    own_rows = own_rows.reshape(obs_total // 2, amplitude.shape[1])
    other_rows = other_rows.reshape(obs_total // 2, amplitude.shape[1])
    shifted = jnp.concatenate([history[:, 1:], jnp.zeros_like(history[:, :1])], axis=1)
    nothing = 0.0 * interp_taps[0, 0, 0]
    def swapped(values, pieces):
        parts = jnp.split(values.astype(jnp.float32), pieces, axis=0)
        parts = [lax.ppermute(part, "space", swap) for part in parts]
        return (jnp.concatenate(parts, axis=0) + nothing).astype(jnp.bfloat16)

    got_signals = swapped(shifted, 4)
    got_rows = swapped(other_rows, 4)
    got_band = lax.ppermute(band_start[0].astype(jnp.float32), "space", swap).astype(jnp.int32)
    got_taps = lax.ppermute(interp_taps[:, 0, :], "space", swap)
    mine = jnp.arange(obs_total // (2 * OB), dtype=jnp.int32)
    mine = 4 * (mine // 2) + 2 * parity + mine % 2
    band_rows = jnp.stack([band_start[0][mine], got_band[mine]])
    tap_rows = jnp.stack([interp_taps[:, 0, :][:, mine], got_taps[:, mine]])
    contract = (((0,), (1,)), ((), ()))
    own_et = lax.dot_general(shifted, own_rows, contract, preferred_element_type=jnp.float32)
    other_et = lax.dot_general(got_signals, got_rows, contract, preferred_element_type=jnp.float32)
    partial = shifted_partial(own_et, other_et, band_rows, tap_rows)
    time_share = lax.psum_scatter(partial, "obs", scatter_dimension=1, tiled=True)
    quarter = time_share.reshape(quads, 2 * OB, time_share.shape[1])
    empty = jnp.zeros_like(quarter)
    pieces = jnp.where(
        parity == 0, jnp.stack([quarter, empty], axis=1), jnp.stack([empty, quarter], axis=1)
    ).reshape(spaces, 2 * OB, time_share.shape[1])
    owner_share = jnp.sum(lax.all_to_all(pieces, "space", 0, 0, tiled=True), axis=0)
    series = lax.all_to_all(owner_share, "obs", split_axis=0, concat_axis=1, tiled=True)

    section = pressure + operator(section_faces(pressure), diffusion)
    pressure_next = 0.5 * (pressure + (section + operator(section_faces(section), diffusion)))
    panel_now = jnp.take(pressure_next.reshape(-1), panel_cell).astype(jnp.bfloat16)

    newest = jnp.dot(amplitude, panel_now, preferred_element_type=jnp.float32).reshape(devices, own)
    per_owner = OB // own
    owner_taps = jnp.repeat(interp_taps[:, 0, :], per_owner, axis=1)
    owner_starts = jnp.repeat(band_start[0].astype(jnp.float32), per_owner)
    payload = jnp.concatenate(
        [
            owner_taps.T[:, :, None] * newest[:, None, :],
            jnp.broadcast_to(owner_starts[:, None, None], (devices, 1, own)),
        ],
        axis=1,
    )
    arrived = lax.all_to_all(payload, axes, 0, 0, tiled=True)
    their_starts = arrived[:, BAND, 0].astype(jnp.int32)
    t_ids = jnp.arange(TS, dtype=jnp.int32)
    for tap_index in range(BAND):
        hit = t_ids[None, :] == (TS - 1 - tap_index - their_starts)[:, None]
        series = series + lax.dot_general(
            arrived[:, tap_index, :],
            hit.astype(jnp.float32),
            (((0,), (0,)), ((), ())),
            precision=lax.Precision.HIGHEST,
        )

    window = 0.5 - 0.5 * jnp.cos(2.0 * math.pi * jnp.arange(TS, dtype=jnp.float32) / TS)
    spectra = dft(series * window[None, :])
    return (pressure_next, panel_now, spectra)


def solution(mesh):
    in_specs = (
        P("space", "obs", None),
        P("space", "obs", None),
        P(("space", "obs")),
        P(("space", "obs"), None),
        P(None, ("space", "obs")),
        P(("space", "obs"), None),
        P(None, ("space", "obs"), None),
    )
    out_specs = (P("space", "obs", None), P(("space", "obs")), P(None, ("space", "obs"), None))
    return jax.shard_map(
        on_device, mesh=mesh, in_specs=in_specs, out_specs=out_specs, check_vma=False
    )
```

```python
import math

import jax
import jax.numpy as jnp
from jax import lax
from jax.experimental import pallas as pl
from jax.experimental.pallas import tpu as pltpu
from jax.sharding import PartitionSpec as P

TS = 2048
BAND = 4
SMAX = 512
OB = 128
NF = 1024
PADR = SMAX + 16
ROWS = 256
T1 = 32
T0 = TS // T1


def with_halo(cells, sides, width):
    for axis, dim in sides:
        count = lax.axis_size(axis)
        ends = count - 1
        head = lax.slice_in_dim(cells, 0, width, axis=dim)
        tail = lax.slice_in_dim(cells, cells.shape[dim] - width, cells.shape[dim], axis=dim)
        cells = jnp.concatenate(
            [
                lax.ppermute(tail, axis, [(i, (i + 1) % count) for i in range(ends)]),
                cells,
                lax.ppermute(head, axis, [((i + 1) % count, i) for i in range(ends)]),
            ],
            axis=dim,
        )
    return cells


def operator(extended, diffusion):
    center = extended[1:-1, 1:-1, :]
    eastward = extended[2:, 1:-1, :]
    westward = extended[:-2, 1:-1, :]
    northward = extended[1:-1, 2:, :]
    southward = extended[1:-1, :-2, :]
    z_padded = jnp.pad(center, ((0, 0), (0, 0), (1, 1)))
    upward = z_padded[:, :, 2:]
    downward = z_padded[:, :, :-2]
    laplace = eastward + westward + northward + southward + upward + downward - 6.0 * center
    return diffusion * laplace - 0.25 * (eastward - westward)


def section_faces(field):
    return with_halo(field, (("space", 0), ("obs", 1)), 1)


def shift_kernel(bs_ref, taps_ref, own_ref, other_ref, out_ref, own_pad, other_pad):
    j = pl.program_id(0)
    for pad_ref, et_ref in ((own_pad, own_ref), (other_pad, other_ref)):
        pad_ref[pl.ds(0, TS), :] = et_ref[...]
        pad_ref[pl.ds(TS, PADR), :] = jnp.zeros((PADR, OB), jnp.float32)
    begins = [bs_ref[0, j], bs_ref[1, j]]
    weights = [[taps_ref[src, k, j] for k in range(BAND)] for src in range(2)]
    for r in range(TS // ROWS):
        acc = None
        for src, pad_ref in enumerate((own_pad, other_pad)):
            for k in range(BAND):
                term = weights[src][k] * pad_ref[pl.ds(begins[src] + k + r * ROWS, ROWS), :]
                acc = term if acc is None else acc + term
        out_ref[:, pl.ds(r * ROWS, ROWS)] = acc.T


def shifted_partial(own_et, other_et, band_rows, taps):
    blocks = own_et.shape[1] // OB
    block_spec = pl.BlockSpec((TS, OB), lambda j, bs: (0, j))
    return pl.pallas_call(
        shift_kernel,
        grid_spec=pltpu.PrefetchScalarGridSpec(
            num_scalar_prefetch=1,
            grid=(blocks,),
            in_specs=[pl.BlockSpec(memory_space=pltpu.SMEM), block_spec, block_spec],
            out_specs=pl.BlockSpec((OB, TS), lambda j, bs: (j, 0)),
            scratch_shapes=[
                pltpu.VMEM((TS + PADR, OB), jnp.float32),
                pltpu.VMEM((TS + PADR, OB), jnp.float32),
            ],
        ),
        out_shape=jax.ShapeDtypeStruct((own_et.shape[1], TS), jnp.float32),
    )(band_rows, taps, own_et, other_et)


def dft(windowed):
    n = windowed.shape[0]
    f_ids = jnp.arange(NF, dtype=jnp.int32)
    t0_ids = jnp.arange(T0, dtype=jnp.int32)
    t1_ids = jnp.arange(T1, dtype=jnp.int32)
    scale = 2.0 * math.pi / TS
    inner = (t0_ids[:, None] * f_ids[None, :] % TS).astype(jnp.float32) * scale
    outer = (t1_ids[:, None] * T0 * f_ids[None, :] % TS).astype(jnp.float32) * scale
    cos_in, sin_in = jnp.cos(inner), jnp.sin(inner)
    cos_out, sin_out = jnp.cos(outer), jnp.sin(outer)
    split = windowed.reshape(n * T1, T0)
    u_cos = jnp.dot(split, cos_in, precision=lax.Precision.HIGHEST).reshape(n, T1, NF)
    u_sin = jnp.dot(split, sin_in, precision=lax.Precision.HIGHEST).reshape(n, T1, NF)
    real_part = jnp.sum(cos_out[None] * u_cos - sin_out[None] * u_sin, axis=1)
    imag_part = -jnp.sum(sin_out[None] * u_cos + cos_out[None] * u_sin, axis=1)
    root = math.sqrt(TS)
    return jnp.stack([real_part / root, imag_part / root])


def on_device(pressure, diffusion, panel_cell, history, amplitude, band_start, interp_taps):
    axes = ("space", "obs")
    devices = lax.axis_size("space") * lax.axis_size("obs")
    obs_total = amplitude.shape[0]
    own = obs_total // devices

    spaces = lax.axis_size("space")
    s_id = lax.axis_index("space")
    parity = s_id % 2
    groups = lax.axis_size("obs")
    ring = 4

    def partner(device):
        s, g = divmod(device, groups)
        z = s % ring
        if g % 2 == 0:
            z = z ^ 1
        else:
            z = (z + 1) % ring if z % 2 else (z - 1) % ring
        return (s - s % ring + z) * groups + g

    swap = [(d, partner(d)) for d in range(spaces * groups)]
    quads = obs_total // (4 * OB)
    halves = amplitude.reshape(quads, 2, 2 * OB, amplitude.shape[1])
    own_rows = lax.dynamic_index_in_dim(halves, parity, axis=1, keepdims=False)
    other_rows = lax.dynamic_index_in_dim(halves, 1 - parity, axis=1, keepdims=False)
    own_rows = own_rows.reshape(obs_total // 2, amplitude.shape[1])
    other_rows = other_rows.reshape(obs_total // 2, amplitude.shape[1])
    shifted = jnp.concatenate([history[:, 1:], jnp.zeros_like(history[:, :1])], axis=1)
    nothing = 0.0 * interp_taps[0, 0, 0]
    def swapped(values, pieces):
        parts = jnp.split(values.astype(jnp.float32), pieces, axis=0)
        parts = [lax.ppermute(part, axes, swap) for part in parts]
        return (jnp.concatenate(parts, axis=0) + nothing).astype(jnp.bfloat16)

    got_signals = swapped(shifted, 4)
    got_rows = swapped(other_rows, 4)
    got_band = lax.ppermute(band_start[0].astype(jnp.float32), axes, swap).astype(jnp.int32)
    got_taps = lax.ppermute(interp_taps[:, 0, :], axes, swap)
    mine = jnp.arange(obs_total // (2 * OB), dtype=jnp.int32)
    mine = 4 * (mine // 2) + 2 * parity + mine % 2
    band_rows = jnp.stack([band_start[0][mine], got_band[mine]])
    tap_rows = jnp.stack([interp_taps[:, 0, :][:, mine], got_taps[:, mine]])
    contract = (((0,), (1,)), ((), ()))
    own_et = lax.dot_general(shifted, own_rows, contract, preferred_element_type=jnp.float32)
    other_et = lax.dot_general(got_signals, got_rows, contract, preferred_element_type=jnp.float32)
    partial = shifted_partial(own_et, other_et, band_rows, tap_rows)
    time_share = lax.psum_scatter(partial, "obs", scatter_dimension=1, tiled=True)
    quarter = time_share.reshape(quads, 2 * OB, time_share.shape[1])
    empty = jnp.zeros_like(quarter)
    pieces = jnp.where(
        parity == 0, jnp.stack([quarter, empty], axis=1), jnp.stack([empty, quarter], axis=1)
    ).reshape(spaces, 2 * OB, time_share.shape[1])
    owner_share = jnp.sum(lax.all_to_all(pieces, "space", 0, 0, tiled=True), axis=0)
    series = lax.all_to_all(owner_share, "obs", split_axis=0, concat_axis=1, tiled=True)

    section = pressure + operator(section_faces(pressure), diffusion)
    pressure_next = 0.5 * (pressure + (section + operator(section_faces(section), diffusion)))
    panel_now = jnp.take(pressure_next.reshape(-1), panel_cell).astype(jnp.bfloat16)

    newest = jnp.dot(amplitude, panel_now, preferred_element_type=jnp.float32).reshape(devices, own)
    per_owner = OB // own
    owner_taps = jnp.repeat(interp_taps[:, 0, :], per_owner, axis=1)
    owner_starts = jnp.repeat(band_start[0].astype(jnp.float32), per_owner)
    payload = jnp.concatenate(
        [
            owner_taps.T[:, :, None] * newest[:, None, :],
            jnp.broadcast_to(owner_starts[:, None, None], (devices, 1, own)),
        ],
        axis=1,
    )
    arrived = lax.all_to_all(payload, axes, 0, 0, tiled=True)
    their_starts = arrived[:, BAND, 0].astype(jnp.int32)
    t_ids = jnp.arange(TS, dtype=jnp.int32)
    for tap_index in range(BAND):
        hit = t_ids[None, :] == (TS - 1 - tap_index - their_starts)[:, None]
        series = series + lax.dot_general(
            arrived[:, tap_index, :],
            hit.astype(jnp.float32),
            (((0,), (0,)), ((), ())),
            precision=lax.Precision.HIGHEST,
        )

    window = 0.5 - 0.5 * jnp.cos(2.0 * math.pi * jnp.arange(TS, dtype=jnp.float32) / TS)
    spectra = dft(series * window[None, :])
    return (pressure_next, panel_now, spectra)


def solution(mesh):
    in_specs = (
        P("space", "obs", None),
        P("space", "obs", None),
        P(("space", "obs")),
        P(("space", "obs"), None),
        P(None, ("space", "obs")),
        P(("space", "obs"), None),
        P(None, ("space", "obs"), None),
    )
    out_specs = (P("space", "obs", None), P(("space", "obs")), P(None, ("space", "obs"), None))
    return jax.shard_map(
        on_device, mesh=mesh, in_specs=in_specs, out_specs=out_specs, check_vma=False
    )
```

```python
import math

import jax
import jax.numpy as jnp
from jax import lax
from jax.experimental import pallas as pl
from jax.experimental.pallas import tpu as pltpu
from jax.sharding import PartitionSpec as P

TS = 2048
BAND = 4
SMAX = 512
OB = 128
NF = 1024
PADR = SMAX + 16
ROWS = 256
T1 = 32
T0 = TS // T1


def with_halo(cells, sides, width):
    for axis, dim in sides:
        count = lax.axis_size(axis)
        ends = count - 1
        head = lax.slice_in_dim(cells, 0, width, axis=dim)
        tail = lax.slice_in_dim(cells, cells.shape[dim] - width, cells.shape[dim], axis=dim)
        cells = jnp.concatenate(
            [
                lax.ppermute(tail, axis, [(i, (i + 1) % count) for i in range(ends)]),
                cells,
                lax.ppermute(head, axis, [((i + 1) % count, i) for i in range(ends)]),
            ],
            axis=dim,
        )
    return cells


def operator(extended, diffusion):
    center = extended[1:-1, 1:-1, :]
    eastward = extended[2:, 1:-1, :]
    westward = extended[:-2, 1:-1, :]
    northward = extended[1:-1, 2:, :]
    southward = extended[1:-1, :-2, :]
    z_padded = jnp.pad(center, ((0, 0), (0, 0), (1, 1)))
    upward = z_padded[:, :, 2:]
    downward = z_padded[:, :, :-2]
    laplace = eastward + westward + northward + southward + upward + downward - 6.0 * center
    return diffusion * laplace - 0.25 * (eastward - westward)


def section_faces(field):
    return with_halo(field, (("space", 0), ("obs", 1)), 1)


def shift_kernel(bs_ref, taps_ref, own_ref, other_ref, out_ref, own_pad, other_pad):
    j = pl.program_id(0)
    for pad_ref, et_ref in ((own_pad, own_ref), (other_pad, other_ref)):
        pad_ref[pl.ds(0, TS), :] = et_ref[...]
        pad_ref[pl.ds(TS, PADR), :] = jnp.zeros((PADR, OB), jnp.float32)
    begins = [bs_ref[0, j], bs_ref[1, j]]
    weights = [[taps_ref[src, k, j] for k in range(BAND)] for src in range(2)]
    for r in range(TS // ROWS):
        acc = None
        for src, pad_ref in enumerate((own_pad, other_pad)):
            for k in range(BAND):
                term = weights[src][k] * pad_ref[pl.ds(begins[src] + k + r * ROWS, ROWS), :]
                acc = term if acc is None else acc + term
        out_ref[:, pl.ds(r * ROWS, ROWS)] = acc.T


def shifted_partial(own_et, other_et, band_rows, taps):
    blocks = own_et.shape[1] // OB
    block_spec = pl.BlockSpec((TS, OB), lambda j, bs: (0, j))
    return pl.pallas_call(
        shift_kernel,
        grid_spec=pltpu.PrefetchScalarGridSpec(
            num_scalar_prefetch=1,
            grid=(blocks,),
            in_specs=[pl.BlockSpec(memory_space=pltpu.SMEM), block_spec, block_spec],
            out_specs=pl.BlockSpec((OB, TS), lambda j, bs: (j, 0)),
            scratch_shapes=[
                pltpu.VMEM((TS + PADR, OB), jnp.float32),
                pltpu.VMEM((TS + PADR, OB), jnp.float32),
            ],
        ),
        out_shape=jax.ShapeDtypeStruct((own_et.shape[1], TS), jnp.float32),
    )(band_rows, taps, own_et, other_et)


def dft(windowed):
    n = windowed.shape[0]
    f_ids = jnp.arange(NF, dtype=jnp.int32)
    t0_ids = jnp.arange(T0, dtype=jnp.int32)
    t1_ids = jnp.arange(T1, dtype=jnp.int32)
    scale = 2.0 * math.pi / TS
    inner = (t0_ids[:, None] * f_ids[None, :] % TS).astype(jnp.float32) * scale
    outer = (t1_ids[:, None] * T0 * f_ids[None, :] % TS).astype(jnp.float32) * scale
    cos_in, sin_in = jnp.cos(inner), jnp.sin(inner)
    cos_out, sin_out = jnp.cos(outer), jnp.sin(outer)
    split = windowed.reshape(n * T1, T0)
    u_cos = jnp.dot(split, cos_in, precision=lax.Precision.HIGHEST).reshape(n, T1, NF)
    u_sin = jnp.dot(split, sin_in, precision=lax.Precision.HIGHEST).reshape(n, T1, NF)
    real_part = jnp.sum(cos_out[None] * u_cos - sin_out[None] * u_sin, axis=1)
    imag_part = -jnp.sum(sin_out[None] * u_cos + cos_out[None] * u_sin, axis=1)
    root = math.sqrt(TS)
    return jnp.stack([real_part / root, imag_part / root])


def on_device(pressure, diffusion, panel_cell, history, amplitude, band_start, interp_taps):
    axes = ("space", "obs")
    devices = lax.axis_size("space") * lax.axis_size("obs")
    obs_total = amplitude.shape[0]
    own = obs_total // devices

    spaces = lax.axis_size("space")
    s_id = lax.axis_index("space")
    parity = s_id % 2
    groups = lax.axis_size("obs")
    ring = 4

    def partner(device):
        s, g = divmod(device, groups)
        z = s % ring
        if g % 2 == 0:
            z = z ^ 1
        else:
            z = (z + 1) % ring if z % 2 else (z - 1) % ring
        return (s - s % ring + z) * groups + g

    swap = [(d, partner(d)) for d in range(spaces * groups)]
    quads = obs_total // (4 * OB)
    halves = amplitude.reshape(quads, 2, 2 * OB, amplitude.shape[1])
    own_rows = lax.dynamic_index_in_dim(halves, parity, axis=1, keepdims=False)
    other_rows = lax.dynamic_index_in_dim(halves, 1 - parity, axis=1, keepdims=False)
    own_rows = own_rows.reshape(obs_total // 2, amplitude.shape[1])
    other_rows = other_rows.reshape(obs_total // 2, amplitude.shape[1])
    shifted = jnp.concatenate([history[:, 1:], jnp.zeros_like(history[:, :1])], axis=1)
    nothing = 0.0 * interp_taps[0, 0, 0]
    def swapped(values, pieces):
        parts = jnp.split(values.astype(jnp.float32), pieces, axis=0)
        parts = [lax.ppermute(part, axes, swap) for part in parts]
        return (jnp.concatenate(parts, axis=0) + nothing).astype(jnp.bfloat16)

    got_signals = swapped(shifted, 4)
    got_rows = swapped(other_rows, 4)
    got_band = lax.ppermute(band_start[0].astype(jnp.float32), axes, swap).astype(jnp.int32)
    got_taps = lax.ppermute(interp_taps[:, 0, :], axes, swap)
    mine = jnp.arange(obs_total // (2 * OB), dtype=jnp.int32)
    mine = 4 * (mine // 2) + 2 * parity + mine % 2
    band_rows = jnp.stack([band_start[0][mine], got_band[mine]])
    tap_rows = jnp.stack([interp_taps[:, 0, :][:, mine], got_taps[:, mine]])
    contract = (((0,), (1,)), ((), ()))
    own_et = lax.dot_general(shifted, own_rows, contract, preferred_element_type=jnp.float32)
    other_et = lax.dot_general(got_signals, got_rows, contract, preferred_element_type=jnp.float32)
    partial = shifted_partial(own_et, other_et, band_rows, tap_rows)
    time_share = lax.psum_scatter(partial, "obs", scatter_dimension=1, tiled=True)
    quarter = time_share.reshape(quads, 2 * OB, time_share.shape[1])
    owner_share = lax.dynamic_index_in_dim(quarter, s_id // 2, axis=0, keepdims=False)
    for mask in range(2, spaces, 2):
        piece = lax.dynamic_index_in_dim(quarter, (s_id ^ mask) // 2, axis=0, keepdims=False)
        owner_share = owner_share + lax.ppermute(
            piece, "space", [(i, i ^ mask) for i in range(spaces)]
        )
    series = lax.all_to_all(owner_share, "obs", split_axis=0, concat_axis=1, tiled=True)

    section = pressure + operator(section_faces(pressure), diffusion)
    pressure_next = 0.5 * (pressure + (section + operator(section_faces(section), diffusion)))
    panel_now = jnp.take(pressure_next.reshape(-1), panel_cell).astype(jnp.bfloat16)

    newest = jnp.dot(amplitude, panel_now, preferred_element_type=jnp.float32).reshape(devices, own)
    per_owner = OB // own
    owner_taps = jnp.repeat(interp_taps[:, 0, :], per_owner, axis=1)
    owner_starts = jnp.repeat(band_start[0].astype(jnp.float32), per_owner)
    payload = jnp.concatenate(
        [
            owner_taps.T[:, :, None] * newest[:, None, :],
            jnp.broadcast_to(owner_starts[:, None, None], (devices, 1, own)),
        ],
        axis=1,
    )
    arrived = lax.all_to_all(payload, axes, 0, 0, tiled=True)
    their_starts = arrived[:, BAND, 0].astype(jnp.int32)
    t_ids = jnp.arange(TS, dtype=jnp.int32)
    for tap_index in range(BAND):
        hit = t_ids[None, :] == (TS - 1 - tap_index - their_starts)[:, None]
        series = series + lax.dot_general(
            arrived[:, tap_index, :],
            hit.astype(jnp.float32),
            (((0,), (0,)), ((), ())),
            precision=lax.Precision.HIGHEST,
        )

    window = 0.5 - 0.5 * jnp.cos(2.0 * math.pi * jnp.arange(TS, dtype=jnp.float32) / TS)
    spectra = dft(series * window[None, :])
    return (pressure_next, panel_now, spectra)


def solution(mesh):
    in_specs = (
        P("space", "obs", None),
        P("space", "obs", None),
        P(("space", "obs")),
        P(("space", "obs"), None),
        P(None, ("space", "obs")),
        P(("space", "obs"), None),
        P(None, ("space", "obs"), None),
    )
    out_specs = (P("space", "obs", None), P(("space", "obs")), P(None, ("space", "obs"), None))
    return jax.shard_map(
        on_device, mesh=mesh, in_specs=in_specs, out_specs=out_specs, check_vma=False
    )
```

```python
import math

import jax
import jax.numpy as jnp
from jax import lax
from jax.experimental import pallas as pl
from jax.experimental.pallas import tpu as pltpu
from jax.sharding import PartitionSpec as P

TS = 2048
BAND = 4
SMAX = 512
OB = 128
NF = 1024
PADR = SMAX + 16
ROWS = 256
T1 = 32
T0 = TS // T1


def with_halo(cells, sides, width):
    for axis, dim in sides:
        count = lax.axis_size(axis)
        ends = count - 1
        head = lax.slice_in_dim(cells, 0, width, axis=dim)
        tail = lax.slice_in_dim(cells, cells.shape[dim] - width, cells.shape[dim], axis=dim)
        cells = jnp.concatenate(
            [
                lax.ppermute(tail, axis, [(i, (i + 1) % count) for i in range(ends)]),
                cells,
                lax.ppermute(head, axis, [((i + 1) % count, i) for i in range(ends)]),
            ],
            axis=dim,
        )
    return cells


def operator(extended, diffusion):
    center = extended[1:-1, 1:-1, :]
    eastward = extended[2:, 1:-1, :]
    westward = extended[:-2, 1:-1, :]
    northward = extended[1:-1, 2:, :]
    southward = extended[1:-1, :-2, :]
    z_padded = jnp.pad(center, ((0, 0), (0, 0), (1, 1)))
    upward = z_padded[:, :, 2:]
    downward = z_padded[:, :, :-2]
    laplace = eastward + westward + northward + southward + upward + downward - 6.0 * center
    return diffusion * laplace - 0.25 * (eastward - westward)


def section_faces(field):
    return with_halo(field, (("space", 0), ("obs", 1)), 1)


def shift_kernel(bs_ref, taps_ref, et_ref, *rest):
    *prior, out_ref, pad_ref = rest
    j = pl.program_id(0)
    pad_ref[pl.ds(0, TS), :] = et_ref[...]
    pad_ref[pl.ds(TS, PADR), :] = jnp.zeros((PADR, OB), jnp.float32)
    begin = bs_ref[j]
    weights = [taps_ref[k, j] for k in range(BAND)]
    for r in range(TS // ROWS):
        acc = weights[0] * pad_ref[pl.ds(begin + r * ROWS, ROWS), :]
        for k in range(1, BAND):
            acc = acc + weights[k] * pad_ref[pl.ds(begin + k + r * ROWS, ROWS), :]
        result = acc.T
        if prior:
            result = prior[0][:, pl.ds(r * ROWS, ROWS)] + result
        out_ref[:, pl.ds(r * ROWS, ROWS)] = result


def shifted_partial(et, band_row, taps, prior=None):
    blocks = et.shape[1] // OB
    in_specs = [pl.BlockSpec(memory_space=pltpu.SMEM), pl.BlockSpec((TS, OB), lambda j, bs: (0, j))]
    operands = [band_row, taps, et]
    aliases = {}
    if prior is not None:
        in_specs.append(pl.BlockSpec((OB, TS), lambda j, bs: (j, 0)))
        operands.append(prior)
        aliases = {3: 0}
    return pl.pallas_call(
        shift_kernel,
        grid_spec=pltpu.PrefetchScalarGridSpec(
            num_scalar_prefetch=1,
            grid=(blocks,),
            in_specs=in_specs,
            out_specs=pl.BlockSpec((OB, TS), lambda j, bs: (j, 0)),
            scratch_shapes=[pltpu.VMEM((TS + PADR, OB), jnp.float32)],
        ),
        out_shape=jax.ShapeDtypeStruct((et.shape[1], TS), jnp.float32),
        input_output_aliases=aliases,
    )(*operands)


def dft(windowed):
    n = windowed.shape[0]
    f_ids = jnp.arange(NF, dtype=jnp.int32)
    t0_ids = jnp.arange(T0, dtype=jnp.int32)
    t1_ids = jnp.arange(T1, dtype=jnp.int32)
    scale = 2.0 * math.pi / TS
    inner = (t0_ids[:, None] * f_ids[None, :] % TS).astype(jnp.float32) * scale
    outer = (t1_ids[:, None] * T0 * f_ids[None, :] % TS).astype(jnp.float32) * scale
    cos_in, sin_in = jnp.cos(inner), jnp.sin(inner)
    cos_out, sin_out = jnp.cos(outer), jnp.sin(outer)
    split = windowed.reshape(n * T1, T0)
    u_cos = jnp.dot(split, cos_in, precision=lax.Precision.HIGHEST).reshape(n, T1, NF)
    u_sin = jnp.dot(split, sin_in, precision=lax.Precision.HIGHEST).reshape(n, T1, NF)
    real_part = jnp.sum(cos_out[None] * u_cos - sin_out[None] * u_sin, axis=1)
    imag_part = -jnp.sum(sin_out[None] * u_cos + cos_out[None] * u_sin, axis=1)
    root = math.sqrt(TS)
    return jnp.stack([real_part / root, imag_part / root])


def on_device(pressure, diffusion, panel_cell, history, amplitude, band_start, interp_taps):
    axes = ("space", "obs")
    devices = lax.axis_size("space") * lax.axis_size("obs")
    obs_total = amplitude.shape[0]
    own = obs_total // devices

    spaces = lax.axis_size("space")
    s_id = lax.axis_index("space")
    parity = s_id % 2
    groups = lax.axis_size("obs")
    ring = 4

    def partner(device):
        s, g = divmod(device, groups)
        z = s % ring
        if g % 2 == 0:
            z = z ^ 1
        else:
            z = (z + 1) % ring if z % 2 else (z - 1) % ring
        return (s - s % ring + z) * groups + g

    swap = [(d, partner(d)) for d in range(spaces * groups)]
    quads = obs_total // (4 * OB)
    halves = amplitude.reshape(quads, 2, 2 * OB, amplitude.shape[1])
    own_rows = lax.dynamic_index_in_dim(halves, parity, axis=1, keepdims=False)
    other_rows = lax.dynamic_index_in_dim(halves, 1 - parity, axis=1, keepdims=False)
    own_rows = own_rows.reshape(obs_total // 2, amplitude.shape[1])
    other_rows = other_rows.reshape(obs_total // 2, amplitude.shape[1])
    shifted = jnp.concatenate([history[:, 1:], jnp.zeros_like(history[:, :1])], axis=1)
    nothing = 0.0 * interp_taps[0, 0, 0]
    def swapped(values, pieces):
        parts = jnp.split(values.astype(jnp.float32), pieces, axis=0)
        parts = [lax.ppermute(part, axes, swap) for part in parts]
        return (jnp.concatenate(parts, axis=0) + nothing).astype(jnp.bfloat16)

    got_signals = swapped(shifted, 4)
    got_rows = swapped(other_rows, 4)
    got_band = lax.ppermute(band_start[0].astype(jnp.float32), axes, swap).astype(jnp.int32)
    got_taps = lax.ppermute(interp_taps[:, 0, :], axes, swap)
    mine = jnp.arange(obs_total // (2 * OB), dtype=jnp.int32)
    mine = 4 * (mine // 2) + 2 * parity + mine % 2
    contract = (((0,), (1,)), ((), ()))
    own_et = lax.dot_general(shifted, own_rows, contract, preferred_element_type=jnp.float32)
    partial = shifted_partial(own_et, band_start[0][mine], interp_taps[:, 0, :][:, mine])
    other_et = lax.dot_general(got_signals, got_rows, contract, preferred_element_type=jnp.float32)
    partial = shifted_partial(other_et, got_band[mine], got_taps[:, mine], partial)
    time_share = lax.psum_scatter(partial, "obs", scatter_dimension=1, tiled=True)
    quarter = time_share.reshape(quads, 2 * OB, time_share.shape[1])
    owner_share = lax.dynamic_index_in_dim(quarter, s_id // 2, axis=0, keepdims=False)
    for mask in range(2, spaces, 2):
        piece = lax.dynamic_index_in_dim(quarter, (s_id ^ mask) // 2, axis=0, keepdims=False)
        owner_share = owner_share + lax.ppermute(
            piece, "space", [(i, i ^ mask) for i in range(spaces)]
        )
    series = lax.all_to_all(owner_share, "obs", split_axis=0, concat_axis=1, tiled=True)

    section = pressure + operator(section_faces(pressure), diffusion)
    pressure_next = 0.5 * (pressure + (section + operator(section_faces(section), diffusion)))
    panel_now = jnp.take(pressure_next.reshape(-1), panel_cell).astype(jnp.bfloat16)

    newest = jnp.dot(amplitude, panel_now, preferred_element_type=jnp.float32).reshape(devices, own)
    per_owner = OB // own
    owner_taps = jnp.repeat(interp_taps[:, 0, :], per_owner, axis=1)
    owner_starts = jnp.repeat(band_start[0].astype(jnp.float32), per_owner)
    payload = jnp.concatenate(
        [
            owner_taps.T[:, :, None] * newest[:, None, :],
            jnp.broadcast_to(owner_starts[:, None, None], (devices, 1, own)),
        ],
        axis=1,
    )
    arrived = lax.all_to_all(payload, axes, 0, 0, tiled=True)
    their_starts = arrived[:, BAND, 0].astype(jnp.int32)
    t_ids = jnp.arange(TS, dtype=jnp.int32)
    for tap_index in range(BAND):
        hit = t_ids[None, :] == (TS - 1 - tap_index - their_starts)[:, None]
        series = series + lax.dot_general(
            arrived[:, tap_index, :],
            hit.astype(jnp.float32),
            (((0,), (0,)), ((), ())),
            precision=lax.Precision.HIGHEST,
        )

    window = 0.5 - 0.5 * jnp.cos(2.0 * math.pi * jnp.arange(TS, dtype=jnp.float32) / TS)
    spectra = dft(series * window[None, :])
    return (pressure_next, panel_now, spectra)


def solution(mesh):
    in_specs = (
        P("space", "obs", None),
        P("space", "obs", None),
        P(("space", "obs")),
        P(("space", "obs"), None),
        P(None, ("space", "obs")),
        P(("space", "obs"), None),
        P(None, ("space", "obs"), None),
    )
    out_specs = (P("space", "obs", None), P(("space", "obs")), P(None, ("space", "obs"), None))
    return jax.shard_map(
        on_device, mesh=mesh, in_specs=in_specs, out_specs=out_specs, check_vma=False
    )
```

```python
import math

import jax
import jax.numpy as jnp
from jax import lax
from jax.experimental import pallas as pl
from jax.experimental.pallas import tpu as pltpu
from jax.sharding import PartitionSpec as P

TS = 2048
BAND = 4
SMAX = 512
OB = 128
NF = 1024
PADR = SMAX + 16
ROWS = 256
T1 = 32
T0 = TS // T1


def with_halo(cells, sides, width):
    for axis, dim in sides:
        count = lax.axis_size(axis)
        ends = count - 1
        head = lax.slice_in_dim(cells, 0, width, axis=dim)
        tail = lax.slice_in_dim(cells, cells.shape[dim] - width, cells.shape[dim], axis=dim)
        cells = jnp.concatenate(
            [
                lax.ppermute(tail, axis, [(i, (i + 1) % count) for i in range(ends)]),
                cells,
                lax.ppermute(head, axis, [((i + 1) % count, i) for i in range(ends)]),
            ],
            axis=dim,
        )
    return cells


def operator(extended, diffusion):
    center = extended[1:-1, 1:-1, :]
    eastward = extended[2:, 1:-1, :]
    westward = extended[:-2, 1:-1, :]
    northward = extended[1:-1, 2:, :]
    southward = extended[1:-1, :-2, :]
    z_padded = jnp.pad(center, ((0, 0), (0, 0), (1, 1)))
    upward = z_padded[:, :, 2:]
    downward = z_padded[:, :, :-2]
    laplace = eastward + westward + northward + southward + upward + downward - 6.0 * center
    return diffusion * laplace - 0.25 * (eastward - westward)


def section_faces(field):
    return with_halo(field, (("space", 0), ("obs", 1)), 1)


def shift_kernel(bs_ref, taps_ref, et_ref, *rest):
    *prior, out_ref, pad_ref = rest
    j = pl.program_id(0)
    pad_ref[pl.ds(0, TS), :] = et_ref[...]
    pad_ref[pl.ds(TS, PADR), :] = jnp.zeros((PADR, OB), jnp.float32)
    begin = bs_ref[j]
    weights = [taps_ref[k, j] for k in range(BAND)]
    for r in range(TS // ROWS):
        acc = weights[0] * pad_ref[pl.ds(begin + r * ROWS, ROWS), :]
        for k in range(1, BAND):
            acc = acc + weights[k] * pad_ref[pl.ds(begin + k + r * ROWS, ROWS), :]
        result = acc.T
        if prior:
            result = prior[0][:, pl.ds(r * ROWS, ROWS)] + result
        out_ref[:, pl.ds(r * ROWS, ROWS)] = result


def shifted_partial(et, band_row, taps, prior=None):
    blocks = et.shape[1] // OB
    in_specs = [pl.BlockSpec(memory_space=pltpu.SMEM), pl.BlockSpec((TS, OB), lambda j, bs: (0, j))]
    operands = [band_row, taps, et]
    aliases = {}
    if prior is not None:
        in_specs.append(pl.BlockSpec((OB, TS), lambda j, bs: (j, 0)))
        operands.append(prior)
        aliases = {3: 0}
    return pl.pallas_call(
        shift_kernel,
        grid_spec=pltpu.PrefetchScalarGridSpec(
            num_scalar_prefetch=1,
            grid=(blocks,),
            in_specs=in_specs,
            out_specs=pl.BlockSpec((OB, TS), lambda j, bs: (j, 0)),
            scratch_shapes=[pltpu.VMEM((TS + PADR, OB), jnp.float32)],
        ),
        out_shape=jax.ShapeDtypeStruct((et.shape[1], TS), jnp.float32),
        input_output_aliases=aliases,
    )(*operands)


def dft(windowed):
    n = windowed.shape[0]
    f_ids = jnp.arange(NF, dtype=jnp.int32)
    t0_ids = jnp.arange(T0, dtype=jnp.int32)
    t1_ids = jnp.arange(T1, dtype=jnp.int32)
    scale = 2.0 * math.pi / TS
    inner = (t0_ids[:, None] * f_ids[None, :] % TS).astype(jnp.float32) * scale
    outer = (t1_ids[:, None] * T0 * f_ids[None, :] % TS).astype(jnp.float32) * scale
    cos_in, sin_in = jnp.cos(inner), jnp.sin(inner)
    cos_out, sin_out = jnp.cos(outer), jnp.sin(outer)
    split = windowed.reshape(n * T1, T0)
    u_cos = jnp.dot(split, cos_in, precision=lax.Precision.HIGHEST).reshape(n, T1, NF)
    u_sin = jnp.dot(split, sin_in, precision=lax.Precision.HIGHEST).reshape(n, T1, NF)
    real_part = jnp.sum(cos_out[None] * u_cos - sin_out[None] * u_sin, axis=1)
    imag_part = -jnp.sum(sin_out[None] * u_cos + cos_out[None] * u_sin, axis=1)
    root = math.sqrt(TS)
    return jnp.stack([real_part / root, imag_part / root])


def on_device(pressure, diffusion, panel_cell, history, amplitude, band_start, interp_taps):
    axes = ("space", "obs")
    devices = lax.axis_size("space") * lax.axis_size("obs")
    obs_total = amplitude.shape[0]
    own = obs_total // devices

    spaces = lax.axis_size("space")
    s_id = lax.axis_index("space")
    parity = s_id % 2
    groups = lax.axis_size("obs")
    ring = 4

    def partner(device):
        s, g = divmod(device, groups)
        z = s % ring
        if g % 2 == 0:
            z = z ^ 1
        else:
            z = (z + 1) % ring if z % 2 else (z - 1) % ring
        return (s - s % ring + z) * groups + g

    swap = [(d, partner(d)) for d in range(spaces * groups)]
    quads = obs_total // (4 * OB)
    halves = amplitude.reshape(quads, 2, 2 * OB, amplitude.shape[1])
    own_rows = lax.dynamic_index_in_dim(halves, parity, axis=1, keepdims=False)
    other_rows = lax.dynamic_index_in_dim(halves, 1 - parity, axis=1, keepdims=False)
    own_rows = own_rows.reshape(obs_total // 2, amplitude.shape[1])
    other_rows = other_rows.reshape(obs_total // 2, amplitude.shape[1])
    shifted = jnp.concatenate([history[:, 1:], jnp.zeros_like(history[:, :1])], axis=1)
    nothing = 0.0 * interp_taps[0, 0, 0]
    def swapped(values, pieces):
        parts = jnp.split(values.astype(jnp.float32), pieces, axis=0)
        parts = [lax.ppermute(part, axes, swap) for part in parts]
        return (jnp.concatenate(parts, axis=0) + nothing).astype(jnp.bfloat16)

    got_signals = swapped(shifted, 4)
    got_rows = swapped(other_rows, 4)
    got_band = lax.ppermute(band_start[0].astype(jnp.float32), axes, swap).astype(jnp.int32)
    got_taps = lax.ppermute(interp_taps[:, 0, :], axes, swap)
    mine = jnp.arange(obs_total // (2 * OB), dtype=jnp.int32)
    mine = 4 * (mine // 2) + 2 * parity + mine % 2
    contract = (((0,), (1,)), ((), ()))
    chunks = 2
    span = obs_total // (2 * chunks)
    per = span // OB
    shares = []
    for chunk in range(chunks):
        rows = slice(chunk * span, (chunk + 1) * span)
        blocks = mine[chunk * per:(chunk + 1) * per]
        own_et = lax.dot_general(
            shifted, own_rows[rows], contract, preferred_element_type=jnp.float32
        )
        partial = shifted_partial(own_et, band_start[0][blocks], interp_taps[:, 0, :][:, blocks])
        other_et = lax.dot_general(
            got_signals, got_rows[rows], contract, preferred_element_type=jnp.float32
        )
        partial = shifted_partial(other_et, got_band[blocks], got_taps[:, blocks], partial)
        shares.append(lax.psum_scatter(partial, "obs", scatter_dimension=1, tiled=True))
    time_share = jnp.concatenate(shares, axis=0)
    quarter = time_share.reshape(quads, 2 * OB, time_share.shape[1])
    owner_share = lax.dynamic_index_in_dim(quarter, s_id // 2, axis=0, keepdims=False)
    for mask in range(2, spaces, 2):
        piece = lax.dynamic_index_in_dim(quarter, (s_id ^ mask) // 2, axis=0, keepdims=False)
        owner_share = owner_share + lax.ppermute(
            piece, "space", [(i, i ^ mask) for i in range(spaces)]
        )
    series = lax.all_to_all(owner_share, "obs", split_axis=0, concat_axis=1, tiled=True)

    section = pressure + operator(section_faces(pressure), diffusion)
    pressure_next = 0.5 * (pressure + (section + operator(section_faces(section), diffusion)))
    panel_now = jnp.take(pressure_next.reshape(-1), panel_cell).astype(jnp.bfloat16)

    newest = jnp.dot(amplitude, panel_now, preferred_element_type=jnp.float32).reshape(devices, own)
    per_owner = OB // own
    owner_taps = jnp.repeat(interp_taps[:, 0, :], per_owner, axis=1)
    owner_starts = jnp.repeat(band_start[0].astype(jnp.float32), per_owner)
    payload = jnp.concatenate(
        [
            owner_taps.T[:, :, None] * newest[:, None, :],
            jnp.broadcast_to(owner_starts[:, None, None], (devices, 1, own)),
        ],
        axis=1,
    )
    arrived = lax.all_to_all(payload, axes, 0, 0, tiled=True)
    their_starts = arrived[:, BAND, 0].astype(jnp.int32)
    t_ids = jnp.arange(TS, dtype=jnp.int32)
    for tap_index in range(BAND):
        hit = t_ids[None, :] == (TS - 1 - tap_index - their_starts)[:, None]
        series = series + lax.dot_general(
            arrived[:, tap_index, :],
            hit.astype(jnp.float32),
            (((0,), (0,)), ((), ())),
            precision=lax.Precision.HIGHEST,
        )

    window = 0.5 - 0.5 * jnp.cos(2.0 * math.pi * jnp.arange(TS, dtype=jnp.float32) / TS)
    spectra = dft(series * window[None, :])
    return (pressure_next, panel_now, spectra)


def solution(mesh):
    in_specs = (
        P("space", "obs", None),
        P("space", "obs", None),
        P(("space", "obs")),
        P(("space", "obs"), None),
        P(None, ("space", "obs")),
        P(("space", "obs"), None),
        P(None, ("space", "obs"), None),
    )
    out_specs = (P("space", "obs", None), P(("space", "obs")), P(None, ("space", "obs"), None))
    return jax.shard_map(
        on_device, mesh=mesh, in_specs=in_specs, out_specs=out_specs, check_vma=False
    )
```

```python
import math

import jax
import jax.numpy as jnp
from jax import lax
from jax.experimental import pallas as pl
from jax.experimental.pallas import tpu as pltpu
from jax.sharding import PartitionSpec as P

TS = 2048
BAND = 4
SMAX = 512
OB = 128
NF = 1024
PADR = SMAX + 16
ROWS = 256
T1 = 32
T0 = TS // T1


def with_halo(cells, sides, width):
    for axis, dim in sides:
        count = lax.axis_size(axis)
        ends = count - 1
        head = lax.slice_in_dim(cells, 0, width, axis=dim)
        tail = lax.slice_in_dim(cells, cells.shape[dim] - width, cells.shape[dim], axis=dim)
        cells = jnp.concatenate(
            [
                lax.ppermute(tail, axis, [(i, (i + 1) % count) for i in range(ends)]),
                cells,
                lax.ppermute(head, axis, [((i + 1) % count, i) for i in range(ends)]),
            ],
            axis=dim,
        )
    return cells


def operator(extended, diffusion):
    center = extended[1:-1, 1:-1, :]
    eastward = extended[2:, 1:-1, :]
    westward = extended[:-2, 1:-1, :]
    northward = extended[1:-1, 2:, :]
    southward = extended[1:-1, :-2, :]
    z_padded = jnp.pad(center, ((0, 0), (0, 0), (1, 1)))
    upward = z_padded[:, :, 2:]
    downward = z_padded[:, :, :-2]
    laplace = eastward + westward + northward + southward + upward + downward - 6.0 * center
    return diffusion * laplace - 0.25 * (eastward - westward)


def section_faces(field):
    return with_halo(field, (("space", 0), ("obs", 1)), 1)


def shift_kernel(bs_ref, taps_ref, et_ref, *rest):
    *prior, out_ref, pad_ref = rest
    j = pl.program_id(0)
    pad_ref[pl.ds(0, TS), :] = et_ref[...]

    @pl.when(j == 0)
    def _():
        pad_ref[pl.ds(TS, PADR), :] = jnp.zeros((PADR, OB), jnp.float32)

    begin = bs_ref[j]
    weights = [taps_ref[k, j] for k in range(BAND)]
    for r in range(TS // ROWS):
        acc = weights[0] * pad_ref[pl.ds(begin + r * ROWS, ROWS), :]
        for k in range(1, BAND):
            acc = acc + weights[k] * pad_ref[pl.ds(begin + k + r * ROWS, ROWS), :]
        result = acc.T
        if prior:
            result = prior[0][:, pl.ds(r * ROWS, ROWS)] + result
        out_ref[:, pl.ds(r * ROWS, ROWS)] = result


def shifted_partial(et, band_row, taps, prior=None):
    blocks = et.shape[1] // OB
    in_specs = [pl.BlockSpec(memory_space=pltpu.SMEM), pl.BlockSpec((TS, OB), lambda j, bs: (0, j))]
    operands = [band_row, taps, et]
    aliases = {}
    if prior is not None:
        in_specs.append(pl.BlockSpec((OB, TS), lambda j, bs: (j, 0)))
        operands.append(prior)
        aliases = {3: 0}
    return pl.pallas_call(
        shift_kernel,
        grid_spec=pltpu.PrefetchScalarGridSpec(
            num_scalar_prefetch=1,
            grid=(blocks,),
            in_specs=in_specs,
            out_specs=pl.BlockSpec((OB, TS), lambda j, bs: (j, 0)),
            scratch_shapes=[pltpu.VMEM((TS + PADR, OB), jnp.float32)],
        ),
        out_shape=jax.ShapeDtypeStruct((et.shape[1], TS), jnp.float32),
        input_output_aliases=aliases,
    )(*operands)


def dft(windowed):
    n = windowed.shape[0]
    f_ids = jnp.arange(NF, dtype=jnp.int32)
    t0_ids = jnp.arange(T0, dtype=jnp.int32)
    t1_ids = jnp.arange(T1, dtype=jnp.int32)
    scale = 2.0 * math.pi / TS
    inner = (t0_ids[:, None] * f_ids[None, :] % TS).astype(jnp.float32) * scale
    outer = (t1_ids[:, None] * T0 * f_ids[None, :] % TS).astype(jnp.float32) * scale
    cos_in, sin_in = jnp.cos(inner), jnp.sin(inner)
    cos_out, sin_out = jnp.cos(outer), jnp.sin(outer)
    split = windowed.reshape(n * T1, T0)
    u_cos = jnp.dot(split, cos_in, precision=lax.Precision.HIGHEST).reshape(n, T1, NF)
    u_sin = jnp.dot(split, sin_in, precision=lax.Precision.HIGHEST).reshape(n, T1, NF)
    real_part = jnp.sum(cos_out[None] * u_cos - sin_out[None] * u_sin, axis=1)
    imag_part = -jnp.sum(sin_out[None] * u_cos + cos_out[None] * u_sin, axis=1)
    root = math.sqrt(TS)
    return jnp.stack([real_part / root, imag_part / root])


def on_device(pressure, diffusion, panel_cell, history, amplitude, band_start, interp_taps):
    axes = ("space", "obs")
    devices = lax.axis_size("space") * lax.axis_size("obs")
    obs_total = amplitude.shape[0]
    own = obs_total // devices

    spaces = lax.axis_size("space")
    s_id = lax.axis_index("space")
    parity = s_id % 2
    groups = lax.axis_size("obs")
    ring = 4

    def partner(device):
        s, g = divmod(device, groups)
        z = s % ring
        if g % 2 == 0:
            z = z ^ 1
        else:
            z = (z + 1) % ring if z % 2 else (z - 1) % ring
        return (s - s % ring + z) * groups + g

    swap = [(d, partner(d)) for d in range(spaces * groups)]
    quads = obs_total // (4 * OB)
    halves = amplitude.reshape(quads, 2, 2 * OB, amplitude.shape[1])
    own_rows = lax.dynamic_index_in_dim(halves, parity, axis=1, keepdims=False)
    other_rows = lax.dynamic_index_in_dim(halves, 1 - parity, axis=1, keepdims=False)
    own_rows = own_rows.reshape(obs_total // 2, amplitude.shape[1])
    other_rows = other_rows.reshape(obs_total // 2, amplitude.shape[1])
    shifted = jnp.concatenate([history[:, 1:], jnp.zeros_like(history[:, :1])], axis=1)
    nothing = 0.0 * interp_taps[0, 0, 0]
    def swapped(values, pieces):
        parts = jnp.split(values.astype(jnp.float32), pieces, axis=0)
        parts = [lax.ppermute(part, axes, swap) for part in parts]
        return (jnp.concatenate(parts, axis=0) + nothing).astype(jnp.bfloat16)

    got_signals = swapped(shifted, 4)
    got_rows = swapped(other_rows, 4)
    got_band = lax.ppermute(band_start[0].astype(jnp.float32), axes, swap).astype(jnp.int32)
    got_taps = lax.ppermute(interp_taps[:, 0, :], axes, swap)
    mine = jnp.arange(obs_total // (2 * OB), dtype=jnp.int32)
    mine = 4 * (mine // 2) + 2 * parity + mine % 2
    contract = (((0,), (1,)), ((), ()))
    own_et = lax.dot_general(shifted, own_rows, contract, preferred_element_type=jnp.float32)
    partial = shifted_partial(own_et, band_start[0][mine], interp_taps[:, 0, :][:, mine])
    other_et = lax.dot_general(got_signals, got_rows, contract, preferred_element_type=jnp.float32)
    partial = shifted_partial(other_et, got_band[mine], got_taps[:, mine], partial)
    time_share = lax.psum_scatter(partial, "obs", scatter_dimension=1, tiled=True)
    quarter = time_share.reshape(quads, 2 * OB, time_share.shape[1])
    owner_share = lax.dynamic_index_in_dim(quarter, s_id // 2, axis=0, keepdims=False)
    for mask in range(2, spaces, 2):
        piece = lax.dynamic_index_in_dim(quarter, (s_id ^ mask) // 2, axis=0, keepdims=False)
        owner_share = owner_share + lax.ppermute(
            piece, "space", [(i, i ^ mask) for i in range(spaces)]
        )
    series = lax.all_to_all(owner_share, "obs", split_axis=0, concat_axis=1, tiled=True)

    section = pressure + operator(section_faces(pressure), diffusion)
    pressure_next = 0.5 * (pressure + (section + operator(section_faces(section), diffusion)))
    panel_now = jnp.take(pressure_next.reshape(-1), panel_cell).astype(jnp.bfloat16)

    newest = jnp.dot(amplitude, panel_now, preferred_element_type=jnp.float32).reshape(devices, own)
    per_owner = OB // own
    owner_taps = jnp.repeat(interp_taps[:, 0, :], per_owner, axis=1)
    owner_starts = jnp.repeat(band_start[0].astype(jnp.float32), per_owner)
    payload = jnp.concatenate(
        [
            owner_taps.T[:, :, None] * newest[:, None, :],
            jnp.broadcast_to(owner_starts[:, None, None], (devices, 1, own)),
        ],
        axis=1,
    )
    arrived = lax.all_to_all(payload, axes, 0, 0, tiled=True)
    their_starts = arrived[:, BAND, 0].astype(jnp.int32)
    t_ids = jnp.arange(TS, dtype=jnp.int32)
    for tap_index in range(BAND):
        hit = t_ids[None, :] == (TS - 1 - tap_index - their_starts)[:, None]
        series = series + lax.dot_general(
            arrived[:, tap_index, :],
            hit.astype(jnp.float32),
            (((0,), (0,)), ((), ())),
            precision=lax.Precision.HIGHEST,
        )

    window = 0.5 - 0.5 * jnp.cos(2.0 * math.pi * jnp.arange(TS, dtype=jnp.float32) / TS)
    spectra = dft(series * window[None, :])
    return (pressure_next, panel_now, spectra)


def solution(mesh):
    in_specs = (
        P("space", "obs", None),
        P("space", "obs", None),
        P(("space", "obs")),
        P(("space", "obs"), None),
        P(None, ("space", "obs")),
        P(("space", "obs"), None),
        P(None, ("space", "obs"), None),
    )
    out_specs = (P("space", "obs", None), P(("space", "obs")), P(None, ("space", "obs"), None))
    return jax.shard_map(
        on_device, mesh=mesh, in_specs=in_specs, out_specs=out_specs, check_vma=False
    )
```

```python
import math

import jax
import jax.numpy as jnp
from jax import lax
from jax.experimental import pallas as pl
from jax.experimental.pallas import tpu as pltpu
from jax.sharding import PartitionSpec as P

TS = 2048
BAND = 4
SMAX = 512
OB = 128
NF = 1024
PADR = SMAX + 16
ROWS = 512
T1 = 32
T0 = TS // T1


def with_halo(cells, sides, width):
    for axis, dim in sides:
        count = lax.axis_size(axis)
        ends = count - 1
        head = lax.slice_in_dim(cells, 0, width, axis=dim)
        tail = lax.slice_in_dim(cells, cells.shape[dim] - width, cells.shape[dim], axis=dim)
        cells = jnp.concatenate(
            [
                lax.ppermute(tail, axis, [(i, (i + 1) % count) for i in range(ends)]),
                cells,
                lax.ppermute(head, axis, [((i + 1) % count, i) for i in range(ends)]),
            ],
            axis=dim,
        )
    return cells


def operator(extended, diffusion):
    center = extended[1:-1, 1:-1, :]
    eastward = extended[2:, 1:-1, :]
    westward = extended[:-2, 1:-1, :]
    northward = extended[1:-1, 2:, :]
    southward = extended[1:-1, :-2, :]
    z_padded = jnp.pad(center, ((0, 0), (0, 0), (1, 1)))
    upward = z_padded[:, :, 2:]
    downward = z_padded[:, :, :-2]
    laplace = eastward + westward + northward + southward + upward + downward - 6.0 * center
    return diffusion * laplace - 0.25 * (eastward - westward)


def section_faces(field):
    return with_halo(field, (("space", 0), ("obs", 1)), 1)


def shift_kernel(bs_ref, taps_ref, et_ref, *rest):
    *prior, out_ref, pad_ref = rest
    j = pl.program_id(0)
    pad_ref[pl.ds(0, TS), :] = et_ref[...]

    @pl.when(j == 0)
    def _():
        pad_ref[pl.ds(TS, PADR), :] = jnp.zeros((PADR, OB), jnp.float32)

    begin = bs_ref[j]
    weights = [taps_ref[k, j] for k in range(BAND)]
    for r in range(TS // ROWS):
        acc = weights[0] * pad_ref[pl.ds(begin + r * ROWS, ROWS), :]
        for k in range(1, BAND):
            acc = acc + weights[k] * pad_ref[pl.ds(begin + k + r * ROWS, ROWS), :]
        result = acc.T
        if prior:
            result = prior[0][:, pl.ds(r * ROWS, ROWS)] + result
        out_ref[:, pl.ds(r * ROWS, ROWS)] = result


def shifted_partial(et, band_row, taps, prior=None):
    blocks = et.shape[1] // OB
    in_specs = [pl.BlockSpec(memory_space=pltpu.SMEM), pl.BlockSpec((TS, OB), lambda j, bs: (0, j))]
    operands = [band_row, taps, et]
    aliases = {}
    if prior is not None:
        in_specs.append(pl.BlockSpec((OB, TS), lambda j, bs: (j, 0)))
        operands.append(prior)
        aliases = {3: 0}
    return pl.pallas_call(
        shift_kernel,
        grid_spec=pltpu.PrefetchScalarGridSpec(
            num_scalar_prefetch=1,
            grid=(blocks,),
            in_specs=in_specs,
            out_specs=pl.BlockSpec((OB, TS), lambda j, bs: (j, 0)),
            scratch_shapes=[pltpu.VMEM((TS + PADR, OB), jnp.float32)],
        ),
        out_shape=jax.ShapeDtypeStruct((et.shape[1], TS), jnp.float32),
        input_output_aliases=aliases,
    )(*operands)


def dft(windowed):
    n = windowed.shape[0]
    f_ids = jnp.arange(NF, dtype=jnp.int32)
    t0_ids = jnp.arange(T0, dtype=jnp.int32)
    t1_ids = jnp.arange(T1, dtype=jnp.int32)
    scale = 2.0 * math.pi / TS
    inner = (t0_ids[:, None] * f_ids[None, :] % TS).astype(jnp.float32) * scale
    outer = (t1_ids[:, None] * T0 * f_ids[None, :] % TS).astype(jnp.float32) * scale
    cos_in, sin_in = jnp.cos(inner), jnp.sin(inner)
    cos_out, sin_out = jnp.cos(outer), jnp.sin(outer)
    split = windowed.reshape(n * T1, T0)
    u_cos = jnp.dot(split, cos_in, precision=lax.Precision.HIGHEST).reshape(n, T1, NF)
    u_sin = jnp.dot(split, sin_in, precision=lax.Precision.HIGHEST).reshape(n, T1, NF)
    real_part = jnp.sum(cos_out[None] * u_cos - sin_out[None] * u_sin, axis=1)
    imag_part = -jnp.sum(sin_out[None] * u_cos + cos_out[None] * u_sin, axis=1)
    root = math.sqrt(TS)
    return jnp.stack([real_part / root, imag_part / root])


def on_device(pressure, diffusion, panel_cell, history, amplitude, band_start, interp_taps):
    axes = ("space", "obs")
    devices = lax.axis_size("space") * lax.axis_size("obs")
    obs_total = amplitude.shape[0]
    own = obs_total // devices

    spaces = lax.axis_size("space")
    s_id = lax.axis_index("space")
    parity = s_id % 2
    groups = lax.axis_size("obs")
    ring = 4

    def partner(device):
        s, g = divmod(device, groups)
        z = s % ring
        if g % 2 == 0:
            z = z ^ 1
        else:
            z = (z + 1) % ring if z % 2 else (z - 1) % ring
        return (s - s % ring + z) * groups + g

    swap = [(d, partner(d)) for d in range(spaces * groups)]
    quads = obs_total // (4 * OB)
    halves = amplitude.reshape(quads, 2, 2 * OB, amplitude.shape[1])
    own_rows = lax.dynamic_index_in_dim(halves, parity, axis=1, keepdims=False)
    other_rows = lax.dynamic_index_in_dim(halves, 1 - parity, axis=1, keepdims=False)
    own_rows = own_rows.reshape(obs_total // 2, amplitude.shape[1])
    other_rows = other_rows.reshape(obs_total // 2, amplitude.shape[1])
    shifted = jnp.concatenate([history[:, 1:], jnp.zeros_like(history[:, :1])], axis=1)
    nothing = 0.0 * interp_taps[0, 0, 0]
    def swapped(values, pieces):
        parts = jnp.split(values.astype(jnp.float32), pieces, axis=0)
        parts = [lax.ppermute(part, axes, swap) for part in parts]
        return (jnp.concatenate(parts, axis=0) + nothing).astype(jnp.bfloat16)

    got_signals = swapped(shifted, 4)
    got_rows = swapped(other_rows, 4)
    got_band = lax.ppermute(band_start[0].astype(jnp.float32), axes, swap).astype(jnp.int32)
    got_taps = lax.ppermute(interp_taps[:, 0, :], axes, swap)
    mine = jnp.arange(obs_total // (2 * OB), dtype=jnp.int32)
    mine = 4 * (mine // 2) + 2 * parity + mine % 2
    contract = (((0,), (1,)), ((), ()))
    own_et = lax.dot_general(shifted, own_rows, contract, preferred_element_type=jnp.float32)
    partial = shifted_partial(own_et, band_start[0][mine], interp_taps[:, 0, :][:, mine])
    other_et = lax.dot_general(got_signals, got_rows, contract, preferred_element_type=jnp.float32)
    partial = shifted_partial(other_et, got_band[mine], got_taps[:, mine], partial)
    time_share = lax.psum_scatter(partial, "obs", scatter_dimension=1, tiled=True)
    quarter = time_share.reshape(quads, 2 * OB, time_share.shape[1])
    owner_share = lax.dynamic_index_in_dim(quarter, s_id // 2, axis=0, keepdims=False)
    for mask in range(2, spaces, 2):
        piece = lax.dynamic_index_in_dim(quarter, (s_id ^ mask) // 2, axis=0, keepdims=False)
        owner_share = owner_share + lax.ppermute(
            piece, "space", [(i, i ^ mask) for i in range(spaces)]
        )
    series = lax.all_to_all(owner_share, "obs", split_axis=0, concat_axis=1, tiled=True)

    section = pressure + operator(section_faces(pressure), diffusion)
    pressure_next = 0.5 * (pressure + (section + operator(section_faces(section), diffusion)))
    panel_now = jnp.take(pressure_next.reshape(-1), panel_cell).astype(jnp.bfloat16)

    newest = jnp.dot(amplitude, panel_now, preferred_element_type=jnp.float32).reshape(devices, own)
    per_owner = OB // own
    owner_taps = jnp.repeat(interp_taps[:, 0, :], per_owner, axis=1)
    owner_starts = jnp.repeat(band_start[0].astype(jnp.float32), per_owner)
    payload = jnp.concatenate(
        [
            owner_taps.T[:, :, None] * newest[:, None, :],
            jnp.broadcast_to(owner_starts[:, None, None], (devices, 1, own)),
        ],
        axis=1,
    )
    arrived = lax.all_to_all(payload, axes, 0, 0, tiled=True)
    their_starts = arrived[:, BAND, 0].astype(jnp.int32)
    t_ids = jnp.arange(TS, dtype=jnp.int32)
    for tap_index in range(BAND):
        hit = t_ids[None, :] == (TS - 1 - tap_index - their_starts)[:, None]
        series = series + lax.dot_general(
            arrived[:, tap_index, :],
            hit.astype(jnp.float32),
            (((0,), (0,)), ((), ())),
            precision=lax.Precision.HIGHEST,
        )

    window = 0.5 - 0.5 * jnp.cos(2.0 * math.pi * jnp.arange(TS, dtype=jnp.float32) / TS)
    spectra = dft(series * window[None, :])
    return (pressure_next, panel_now, spectra)


def solution(mesh):
    in_specs = (
        P("space", "obs", None),
        P("space", "obs", None),
        P(("space", "obs")),
        P(("space", "obs"), None),
        P(None, ("space", "obs")),
        P(("space", "obs"), None),
        P(None, ("space", "obs"), None),
    )
    out_specs = (P("space", "obs", None), P(("space", "obs")), P(None, ("space", "obs"), None))
    return jax.shard_map(
        on_device, mesh=mesh, in_specs=in_specs, out_specs=out_specs, check_vma=False
    )
```
